32 devices in a mesh: grp: 4 (over y, core), blk: 8 (over z, x).
Axes of the slice: x: 2, y: 2, z: 4, core: 2. Of those that a mesh axis runs over, the one named last changes fastest.
Arguments:
- embeddings: bfloat16 [2048, 4096], P(('grp', 'blk'))
- cluster_ids: int32 [2048], P(('grp', 'blk')), may hold values from 0 to 3, as said below
- row_index: int32 [2048], P(('grp', 'blk')), may hold values from 0 to 2047, each once
Outputs:
- best_similarity: float32 [2048], P(('grp', 'blk'))
The draws below stay inside these ranges and needn't reach their ends.
Inputs may be any that keep to these rules, and one draw needn't show every extreme that they name: The owner group of a row is cluster_ids mod 4 (the number of devices along grp). Among the rows of one device at most 38 have one owner group; in every draw some device has exactly 38 rows of one group, and for some index along blk all devices along grp have exactly 38 rows of the same group. `row_index`: each number appears once.
All inputs are finite; a program needn't handle non-finite values.
Results may differ from the reference program's by a relative error of at most 0.00038.
Values may be sent and summed in bfloat16 or wider, within the bound.
No kernel may reach another device: no remote copies, remote signals or barrier semaphores. Data moves between devices by JAX's collectives and lax.ppermute only.
A program may use at most 64 MiB of HBM per device.

```python
import math
import jax
import jax.numpy as jnp
from jax import lax

D = 4096
ROWS_DEV = 64
CPG = 1
CAP = 38
CLUSTERS = 4
ROWS = 2048
N_GRP = 4
N_BLK = 8


def shuffle_one(subkey):
    return jax.random.permutation(subkey, ROWS_DEV)


def cluster_table(base):
    block_count = N_GRP * N_BLK
    subkeys = jax.random.split(base, 8)
    busy_group = jax.random.randint(subkeys[0], (block_count,), 0, N_GRP)
    busy_count = CAP - jax.random.randint(subkeys[1], (block_count,), 0, CAP // 3 + 1)
    chosen_blk = jax.random.randint(subkeys[2], (), 0, N_BLK)
    chosen_group = jax.random.randint(subkeys[3], (), 0, N_GRP)
    chosen = jnp.arange(block_count) % N_BLK == chosen_blk
    busy_group = jnp.where(chosen, chosen_group, busy_group)
    busy_count = jnp.where(chosen, CAP, busy_count)
    shuffled = jax.vmap(shuffle_one)(jax.random.split(subkeys[4], block_count))
    elsewhere = (busy_group[:, None] + 1 + jax.random.randint(subkeys[5], (block_count, ROWS_DEV), 0, N_GRP - 1)) % N_GRP
    owner = jnp.where(shuffled < busy_count[:, None], busy_group[:, None], elsewhere)
    first_draw = jax.random.randint(subkeys[6], (block_count, ROWS_DEV), 0, CPG)
    second_draw = jax.random.randint(subkeys[7], (block_count, ROWS_DEV), 0, CPG)
    third_draw = jax.random.randint(jax.random.fold_in(base, 5), (block_count, ROWS_DEV), 0, CPG)
    within = jnp.minimum(jnp.minimum(first_draw, second_draw), third_draw)
    return (owner + N_GRP * within).reshape(-1).astype(jnp.int32)


def draw_cluster_ids(key, part):
    return cluster_table(jax.random.fold_in(key, 17))


def draw_embeddings(key, part):
    clusters = cluster_table(jax.random.fold_in(key, 17))
    subkeys = jax.random.split(jax.random.fold_in(key, 23), 2)
    centers = jax.random.normal(subkeys[0], (CLUSTERS, D), jnp.float32)
    noise = jax.random.normal(subkeys[1], (ROWS, D), jnp.float32)
    return (noise + 0.8 * centers[clusters]).astype(jnp.bfloat16)


def setup_inputs(seed: int = 0) -> dict:
    seeds = jax.random.split(jax.random.key(seed), 4)
    return {
        "embeddings": draw_embeddings(jax.random.fold_in(seeds[3], 71), 0),
        "cluster_ids": draw_cluster_ids(jax.random.fold_in(seeds[3], 71), 0),
        "row_index": jax.random.permutation(seeds[2], ROWS).astype(jnp.int32),
    }


def reference(embeddings, cluster_ids, row_index):
    widened = embeddings.astype(jnp.float32)
    square_sum = lax.optimization_barrier(jnp.sum(widened * widened, axis=1, keepdims=True))
    unit_rows = (widened * lax.rsqrt(square_sum / D + 1e-06) / math.sqrt(D)).astype(jnp.bfloat16)
    block_width = ROWS // N_GRP

    def one_block(row_start):
        block_rows = lax.dynamic_slice_in_dim(unit_rows, row_start, block_width, 0)
        block_clusters = lax.dynamic_slice_in_dim(cluster_ids, row_start, block_width, 0)
        block_index = lax.dynamic_slice_in_dim(row_index, row_start, block_width, 0)
        scores = jnp.einsum('id,jd->ij', block_rows, unit_rows, preferred_element_type=jnp.float32)
        earlier = (block_clusters[:, None] == cluster_ids[None, :]) & (row_index[None, :] < block_index[:, None])
        return lax.optimization_barrier(jnp.max(jnp.where(earlier, scores, jnp.float32(-1.0)), axis=1))
    starts = (jnp.arange(N_GRP) * block_width).astype(jnp.int32)
    return lax.map(one_block, starts).reshape(ROWS)
```

```python
import math

import jax
import jax.numpy as jnp
from jax import lax
from jax.sharding import PartitionSpec as P

D = 4096
LABEL_SHIFT = 65536


def per_device(embeddings, cluster_ids, row_index):
    group_count = lax.axis_size("grp")
    widened = embeddings.astype(jnp.float32)
    square_sum = jnp.sum(widened * widened, axis=1, keepdims=True)
    unit_rows = (widened * lax.rsqrt(square_sum / D + 1e-06) / math.sqrt(D)).astype(jnp.bfloat16)
    labels = cluster_ids * LABEL_SHIFT + row_index

    left_rows = lax.all_gather(unit_rows, "grp", axis=0, tiled=True)
    left_labels = lax.all_gather(labels, "grp", axis=0, tiled=True)
    right_rows = lax.all_gather(unit_rows, "blk", axis=0, tiled=True)
    right_labels = lax.all_gather(labels, "blk", axis=0, tiled=True)

    scores = jnp.einsum("id,jd->ij", left_rows, right_rows, preferred_element_type=jnp.float32)
    same_cluster = (left_labels[:, None] // LABEL_SHIFT) == (right_labels[None, :] // LABEL_SHIFT)
    earlier = same_cluster & (right_labels[None, :] < left_labels[:, None])
    partial = jnp.max(jnp.where(earlier, scores, jnp.float32(-1.0)), axis=1)

    partial = partial.reshape(group_count, -1)
    gathered = lax.all_to_all(partial, "grp", split_axis=0, concat_axis=0, tiled=True)
    return jnp.max(gathered, axis=0)


def solution(mesh):
    return jax.shard_map(
        per_device,
        mesh=mesh,
        in_specs=(P(("grp", "blk"), None), P(("grp", "blk")), P(("grp", "blk"))),
        out_specs=P(("grp", "blk")),
        check_vma=False,
    )
```

```python
import math

import jax
import jax.numpy as jnp
from jax import lax
from jax.sharding import PartitionSpec as P

D = 4096
LABEL_SHIFT = 65536.0


def ring_order(count):
    if count % 2:
        return list(range(count))
    return [2 * k for k in range(count // 2)] + [2 * k + 1 for k in reversed(range(count // 2))]


def per_device(embeddings, cluster_ids, row_index):
    group_count = lax.axis_size("grp")
    block_count = lax.axis_size("blk")
    widened = embeddings.astype(jnp.float32)
    square_sum = jnp.sum(widened * widened, axis=1, keepdims=True)
    unit_rows = (widened * lax.rsqrt(square_sum / D + 1e-06) / math.sqrt(D)).astype(jnp.bfloat16)
    labels = cluster_ids.astype(jnp.float32) * LABEL_SHIFT + row_index.astype(jnp.float32)

    left_rows = lax.all_gather(unit_rows, "grp", axis=0, tiled=True)
    left_labels = lax.all_gather(labels, "grp", axis=0, tiled=True)

    order = ring_order(block_count)
    forward = [(order[i], order[(i + 1) % block_count]) for i in range(block_count)]
    backward = [(dst, src) for src, dst in forward]
    ahead, behind = (unit_rows, labels), (unit_rows, labels)
    blocks = [(unit_rows, labels)]
    for step in range(block_count // 2):
        ahead = lax.ppermute(ahead, "blk", forward)
        blocks.append(ahead)
        if step < (block_count - 1) // 2:
            behind = lax.ppermute(behind, "blk", backward)
            blocks.append(behind)
    right_rows = jnp.concatenate([rows for rows, _ in blocks], axis=0)
    right_labels = jnp.concatenate([lab for _, lab in blocks], axis=0)

    scores = jnp.einsum("id,jd->ij", left_rows, right_rows, preferred_element_type=jnp.float32)
    same_cluster = jnp.floor(left_labels[:, None] / LABEL_SHIFT) == jnp.floor(right_labels[None, :] / LABEL_SHIFT)
    earlier = same_cluster & (right_labels[None, :] < left_labels[:, None])
    partial = jnp.max(jnp.where(earlier, scores, jnp.float32(-1.0)), axis=1)

    partial = partial.reshape(group_count, -1)
    gathered = lax.all_to_all(partial, "grp", split_axis=0, concat_axis=0, tiled=True)
    return jnp.max(gathered, axis=0)


def solution(mesh):
    return jax.shard_map(
        per_device,
        mesh=mesh,
        in_specs=(P(("grp", "blk"), None), P(("grp", "blk")), P(("grp", "blk"))),
        out_specs=P(("grp", "blk")),
        check_vma=False,
    )
```

```python
import math

import jax
import jax.numpy as jnp
from jax import lax
from jax.sharding import PartitionSpec as P

D = 4096
LABEL_SHIFT = 65536.0


def ring_order(count):
    if count % 2:
        return list(range(count))
    return [2 * k for k in range(count // 2)] + [2 * k + 1 for k in reversed(range(count // 2))]


def block_best(left_rows, left_labels, right_rows, right_labels):
    scores = jnp.einsum("id,jd->ij", left_rows, right_rows, preferred_element_type=jnp.float32)
    same_cluster = jnp.floor(left_labels[:, None] / LABEL_SHIFT) == jnp.floor(right_labels[None, :] / LABEL_SHIFT)
    earlier = same_cluster & (right_labels[None, :] < left_labels[:, None])
    return jnp.max(jnp.where(earlier, scores, jnp.float32(-1.0)), axis=1)


def per_device(embeddings, cluster_ids, row_index):
    group_count = lax.axis_size("grp")
    block_count = lax.axis_size("blk")
    rows_here = embeddings.shape[0]
    widened = embeddings.astype(jnp.float32)
    square_sum = jnp.sum(widened * widened, axis=1, keepdims=True)
    unit_rows = (widened * lax.rsqrt(square_sum / D + 1e-06) / math.sqrt(D)).astype(jnp.bfloat16)
    labels = cluster_ids.astype(jnp.float32) * LABEL_SHIFT + row_index.astype(jnp.float32)

    all_labels = lax.all_gather(labels, ("grp", "blk"), axis=0, tiled=True)
    all_labels = all_labels.reshape(group_count, block_count, rows_here)
    my_grp = lax.axis_index("grp")
    my_blk = lax.axis_index("blk")
    left_labels = lax.dynamic_index_in_dim(all_labels, my_blk, axis=1, keepdims=False).reshape(-1)
    my_column = lax.dynamic_index_in_dim(all_labels, my_grp, axis=0, keepdims=False)
    left_rows = lax.all_gather(unit_rows, "grp", axis=0, tiled=True)

    order = ring_order(block_count)
    place = [0] * block_count
    for position, blk in enumerate(order):
        place[blk] = position
    order_table = jnp.array(order, jnp.int32)
    my_place = jnp.array(place, jnp.int32)[my_blk]

    def column_labels(shift):
        source = order_table[(my_place + shift) % block_count]
        return lax.dynamic_index_in_dim(my_column, source, axis=0, keepdims=False)

    forward = [(order[i], order[(i + 1) % block_count]) for i in range(block_count)]
    backward = [(dst, src) for src, dst in forward]
    best = block_best(left_rows, left_labels, unit_rows, labels)
    ahead, behind = unit_rows, unit_rows
    for step in range(1, block_count // 2 + 1):
        ahead = lax.ppermute(ahead, "blk", forward)
        best = jnp.maximum(best, block_best(left_rows, left_labels, ahead, column_labels(-step)))
        if step <= (block_count - 1) // 2:
            behind = lax.ppermute(behind, "blk", backward)
            best = jnp.maximum(best, block_best(left_rows, left_labels, behind, column_labels(step)))

    best = best.reshape(group_count, rows_here)
    result = lax.dynamic_index_in_dim(best, my_grp, axis=0, keepdims=False)
    for shift in range(1, group_count):
        target = (my_grp + shift) % group_count
        piece = lax.dynamic_index_in_dim(best, target, axis=0, keepdims=False)
        pairs = [(g, (g + shift) % group_count) for g in range(group_count)]
        result = jnp.maximum(result, lax.ppermute(piece, "grp", pairs))
    return result


def solution(mesh):
    return jax.shard_map(
        per_device,
        mesh=mesh,
        in_specs=(P(("grp", "blk"), None), P(("grp", "blk")), P(("grp", "blk"))),
        out_specs=P(("grp", "blk")),
        check_vma=False,
    )
```

```python
import math

import jax
import jax.numpy as jnp
from jax import lax
from jax.sharding import PartitionSpec as P

D = 4096
TAG_WIDTH = 128
ORDER_SPAN = 8192.0


def ring_order(count):
    if count % 2:
        return list(range(count))
    return [2 * k for k in range(count // 2)] + [2 * k + 1 for k in reversed(range(count // 2))]


def tag_labels(payload):
    high = payload[:, D].astype(jnp.float32)
    low = payload[:, D + 1].astype(jnp.float32)
    return high * 128.0 + low


def block_best(left_rows, left_labels, payload):
    scores = jnp.einsum("id,jd->ij", left_rows, payload, preferred_element_type=jnp.float32)
    right_labels = tag_labels(payload)
    same_cluster = jnp.floor(left_labels[:, None] / ORDER_SPAN) == jnp.floor(right_labels[None, :] / ORDER_SPAN)
    earlier = same_cluster & (right_labels[None, :] < left_labels[:, None])
    return jnp.max(jnp.where(earlier, scores, jnp.float32(-1.0)), axis=1)


def per_device(embeddings, cluster_ids, row_index):
    group_count = lax.axis_size("grp")
    block_count = lax.axis_size("blk")
    rows_here = embeddings.shape[0]
    widened = embeddings.astype(jnp.float32)
    square_sum = jnp.sum(widened * widened, axis=1, keepdims=True)
    unit_rows = (widened * lax.rsqrt(square_sum / D + 1e-06) / math.sqrt(D)).astype(jnp.bfloat16)
    high = cluster_ids * 64 + row_index // 128
    low = row_index % 128
    column = jnp.arange(TAG_WIDTH)[None, :]
    tags = jnp.where(column == 0, high[:, None], jnp.where(column == 1, low[:, None], 0)).astype(jnp.bfloat16)
    payload = jnp.concatenate([unit_rows, tags], axis=1)

    left_payload = lax.all_gather(payload, "grp", axis=0, tiled=True)
    left_labels = tag_labels(left_payload)
    inside = jnp.arange(D + TAG_WIDTH)[None, :] < D
    left_rows = jnp.where(inside, left_payload, jnp.zeros_like(left_payload))

    order = ring_order(block_count)
    forward = [(order[i], order[(i + 1) % block_count]) for i in range(block_count)]
    backward = [(dst, src) for src, dst in forward]
    best = block_best(left_rows, left_labels, payload)
    ahead, behind = payload, payload
    for step in range(1, block_count // 2 + 1):
        ahead = lax.ppermute(ahead, "blk", forward)
        best = jnp.maximum(best, block_best(left_rows, left_labels, ahead))
        if step <= (block_count - 1) // 2:
            behind = lax.ppermute(behind, "blk", backward)
            best = jnp.maximum(best, block_best(left_rows, left_labels, behind))

    my_grp = lax.axis_index("grp")
    best = best.reshape(group_count, rows_here)
    result = lax.dynamic_index_in_dim(best, my_grp, axis=0, keepdims=False)
    for shift in range(1, group_count):
        target = (my_grp + shift) % group_count
        piece = lax.dynamic_index_in_dim(best, target, axis=0, keepdims=False)
        pairs = [(g, (g + shift) % group_count) for g in range(group_count)]
        result = jnp.maximum(result, lax.ppermute(piece, "grp", pairs))
    return result


def solution(mesh):
    return jax.shard_map(
        per_device,
        mesh=mesh,
        in_specs=(P(("grp", "blk"), None), P(("grp", "blk")), P(("grp", "blk"))),
        out_specs=P(("grp", "blk")),
        check_vma=False,
    )
```

```python
import math

import jax
import jax.numpy as jnp
from jax import lax
from jax.sharding import PartitionSpec as P

D = 4096
TAG_WIDTH = 128
ORDER_SPAN = 8192.0


def ring_order(count):
    if count % 2:
        return list(range(count))
    return [2 * k for k in range(count // 2)] + [2 * k + 1 for k in reversed(range(count // 2))]


def tag_labels(payload):
    high = payload[:, D].astype(jnp.float32)
    low = payload[:, D + 1].astype(jnp.float32)
    return high * 128.0 + low


def block_best(left_rows, left_labels, payload):
    scores = jnp.einsum("id,jd->ij", left_rows, payload, preferred_element_type=jnp.float32)
    right_labels = tag_labels(payload)
    same_cluster = jnp.floor(left_labels[:, None] / ORDER_SPAN) == jnp.floor(right_labels[None, :] / ORDER_SPAN)
    earlier = same_cluster & (right_labels[None, :] < left_labels[:, None])
    return jnp.max(jnp.where(earlier, scores, jnp.float32(-1.0)), axis=1)


def partner_pairs(group_count, mask):
    return [(g, g ^ mask) for g in range(group_count)]


def per_device(embeddings, cluster_ids, row_index):
    group_count = lax.axis_size("grp")
    block_count = lax.axis_size("blk")
    rows_here = embeddings.shape[0]
    widened = embeddings.astype(jnp.float32)
    square_sum = jnp.sum(widened * widened, axis=1, keepdims=True)
    unit_rows = (widened * lax.rsqrt(square_sum / D + 1e-06) / math.sqrt(D)).astype(jnp.bfloat16)
    high = cluster_ids * 64 + row_index // 128
    low = row_index % 128
    column = jnp.arange(TAG_WIDTH)[None, :]
    tags = jnp.where(column == 0, high[:, None], jnp.where(column == 1, low[:, None], 0)).astype(jnp.bfloat16)
    payload = jnp.concatenate([unit_rows, tags], axis=1)

    if group_count == 4:
        across = lax.ppermute(payload, "grp", partner_pairs(group_count, 2))
        beside = lax.ppermute(payload, "grp", partner_pairs(group_count, 1))
        diagonal = lax.ppermute(across, "grp", partner_pairs(group_count, 1))
        segment_pairs = [partner_pairs(group_count, k) for k in range(1, 4)]
        left_payload = jnp.concatenate([payload, beside, across, diagonal], axis=0)
    else:
        shifted = [lax.ppermute(payload, "grp", [(g, (g + k) % group_count) for g in range(group_count)])
                   for k in range(1, group_count)]
        segment_pairs = [[(g, (g - k) % group_count) for g in range(group_count)] for k in range(1, group_count)]
        left_payload = jnp.concatenate([payload] + shifted, axis=0)
    left_labels = tag_labels(left_payload)
    inside = jnp.arange(D + TAG_WIDTH)[None, :] < D
    left_rows = jnp.where(inside, left_payload, jnp.zeros_like(left_payload))

    order = ring_order(block_count)
    forward = [(order[i], order[(i + 1) % block_count]) for i in range(block_count)]
    backward = [(dst, src) for src, dst in forward]
    best = None
    pending = [payload]
    ahead, behind = payload, payload
    for step in range(1, block_count // 2 + 1):
        ahead = lax.ppermute(ahead, "blk", forward)
        stepped = [ahead]
        if step <= (block_count - 1) // 2:
            behind = lax.ppermute(behind, "blk", backward)
            stepped.append(behind)
        if step >= 2:
            for block in pending:
                tile = block_best(left_rows, left_labels, block)
                best = tile if best is None else jnp.maximum(best, tile)
            pending = []
            stepped, best = lax.optimization_barrier((stepped, best))
            ahead = stepped[0]
            if len(stepped) > 1:
                behind = stepped[1]
        pending.extend(stepped)
    for block in pending:
        tile = block_best(left_rows, left_labels, block)
        best = tile if best is None else jnp.maximum(best, tile)

    best = best.reshape(group_count, rows_here)
    result = best[0]
    for k, pairs in enumerate(segment_pairs, start=1):
        result = jnp.maximum(result, lax.ppermute(best[k], "grp", pairs))
    return result


def solution(mesh):
    return jax.shard_map(
        per_device,
        mesh=mesh,
        in_specs=(P(("grp", "blk"), None), P(("grp", "blk")), P(("grp", "blk"))),
        out_specs=P(("grp", "blk")),
        check_vma=False,
    )
```

```python
import math

import jax
import jax.numpy as jnp
from jax import lax
from jax.sharding import PartitionSpec as P

D = 4096
TAG_WIDTH = 128
ORDER_SPAN = 8192.0


def ring_order(count):
    if count % 2:
        return list(range(count))
    return [2 * k for k in range(count // 2)] + [2 * k + 1 for k in reversed(range(count // 2))]


def tag_labels(payload):
    high = payload[:, D].astype(jnp.float32)
    low = payload[:, D + 1].astype(jnp.float32)
    return high * 128.0 + low


def block_best(left_rows, left_labels, payload):
    scores = jnp.einsum("id,jd->ij", left_rows, payload, preferred_element_type=jnp.float32)
    right_labels = tag_labels(payload)
    same_cluster = jnp.floor(left_labels[:, None] / ORDER_SPAN) == jnp.floor(right_labels[None, :] / ORDER_SPAN)
    earlier = same_cluster & (right_labels[None, :] < left_labels[:, None])
    return jnp.max(jnp.where(earlier, scores, jnp.float32(-1.0)), axis=1)


def partner_pairs(group_count, mask):
    return [(g, g ^ mask) for g in range(group_count)]


def per_device(embeddings, cluster_ids, row_index):
    group_count = lax.axis_size("grp")
    block_count = lax.axis_size("blk")
    rows_here = embeddings.shape[0]
    widened = embeddings.astype(jnp.float32)
    square_sum = jnp.sum(widened * widened, axis=1, keepdims=True)
    unit_rows = (widened * lax.rsqrt(square_sum / D + 1e-06) / math.sqrt(D)).astype(jnp.bfloat16)
    high = cluster_ids * 64 + row_index // 128
    low = row_index % 128
    column = jnp.arange(TAG_WIDTH)[None, :]
    tags = jnp.where(column == 0, high[:, None], jnp.where(column == 1, low[:, None], 0)).astype(jnp.bfloat16)
    payload = jnp.concatenate([unit_rows, tags], axis=1)

    if group_count == 4:
        across = lax.ppermute(payload, "grp", partner_pairs(group_count, 2))
        beside = lax.ppermute(payload, "grp", partner_pairs(group_count, 1))
        diagonal = lax.ppermute(across, "grp", partner_pairs(group_count, 1))
        segment_pairs = [partner_pairs(group_count, k) for k in range(1, 4)]
        left_payload = jnp.concatenate([payload, beside, across, diagonal], axis=0)
    else:
        shifted = [lax.ppermute(payload, "grp", [(g, (g + k) % group_count) for g in range(group_count)])
                   for k in range(1, group_count)]
        segment_pairs = [[(g, (g - k) % group_count) for g in range(group_count)] for k in range(1, group_count)]
        left_payload = jnp.concatenate([payload] + shifted, axis=0)
    left_labels = tag_labels(left_payload)
    inside = jnp.arange(D + TAG_WIDTH)[None, :] < D
    left_rows = jnp.where(inside, left_payload, jnp.zeros_like(left_payload))

    order = ring_order(block_count)
    forward = [(order[i], order[(i + 1) % block_count]) for i in range(block_count)]
    backward = [(dst, src) for src, dst in forward]
    half = rows_here // 2

    def fold(best, blocks):
        for block in blocks:
            tile = block_best(left_rows, left_labels, block)
            best = tile if best is None else jnp.maximum(best, tile)
        return best

    chains = [[payload, forward, None, [payload]], [payload, backward, None, []]]
    steps = block_count // 2
    for step in range(1, steps + 1):
        for which, chain in enumerate(chains):
            visiting, pairs, best, pending = chain
            if step == steps and block_count % 2 == 0:
                visiting = visiting[:half] if which == 0 else visiting[half:]
            visiting = lax.ppermute(visiting, "blk", pairs)
            if step >= 2:
                best = fold(best, pending)
                pending = []
                visiting, best = lax.optimization_barrier((visiting, best))
            pending.append(visiting)
            chain[0], chain[2], chain[3] = visiting, best, pending
    best = None
    for _, _, chain_best, pending in chains:
        chain_best = fold(chain_best, pending)
        if chain_best is not None:
            best = chain_best if best is None else jnp.maximum(best, chain_best)

    best = best.reshape(group_count, rows_here)
    result = best[0]
    for k, pairs in enumerate(segment_pairs, start=1):
        result = jnp.maximum(result, lax.ppermute(best[k], "grp", pairs))
    return result


def solution(mesh):
    return jax.shard_map(
        per_device,
        mesh=mesh,
        in_specs=(P(("grp", "blk"), None), P(("grp", "blk")), P(("grp", "blk"))),
        out_specs=P(("grp", "blk")),
        check_vma=False,
    )
```

```python
import math

import jax
import jax.numpy as jnp
from jax import lax
from jax.sharding import PartitionSpec as P

D = 4096
TAG_WIDTH = 128
ORDER_SPAN = 8192.0


def ring_order(count):
    if count % 2:
        return list(range(count))
    return [2 * k for k in range(count // 2)] + [2 * k + 1 for k in reversed(range(count // 2))]


def tag_labels(payload):
    high = payload[:, D].astype(jnp.float32)
    low = payload[:, D + 1].astype(jnp.float32)
    return high * 128.0 + low


def block_best(left_rows, left_labels, payload):
    scores = jnp.einsum("id,jd->ij", left_rows, payload[:, :D], preferred_element_type=jnp.float32)
    right_labels = tag_labels(payload)
    same_cluster = jnp.floor(left_labels[:, None] / ORDER_SPAN) == jnp.floor(right_labels[None, :] / ORDER_SPAN)
    earlier = same_cluster & (right_labels[None, :] < left_labels[:, None])
    return jnp.max(jnp.where(earlier, scores, jnp.float32(-1.0)), axis=1)


def partner_pairs(group_count, mask):
    return [(g, g ^ mask) for g in range(group_count)]


def per_device(embeddings, cluster_ids, row_index):
    group_count = lax.axis_size("grp")
    block_count = lax.axis_size("blk")
    rows_here = embeddings.shape[0]
    widened = embeddings.astype(jnp.float32)
    square_sum = jnp.sum(widened * widened, axis=1, keepdims=True)
    scale = lax.rsqrt(square_sum / D + 1e-06)
    high = (cluster_ids * 64 + row_index // 128).astype(jnp.float32)[:, None]
    low = (row_index % 128).astype(jnp.float32)[:, None]
    column = jnp.arange(D + TAG_WIDTH)[None, :]
    padded = jnp.pad(widened, ((0, 0), (0, TAG_WIDTH)))
    tags = jnp.where(column == D, high, jnp.where(column == D + 1, low, 0.0))
    payload = jnp.where(column < D, padded * scale / math.sqrt(D), tags).astype(jnp.bfloat16)

    order = ring_order(block_count)
    forward = [(order[i], order[(i + 1) % block_count]) for i in range(block_count)]
    backward = [(dst, src) for src, dst in forward]
    half = rows_here // 2
    steps = block_count // 2

    def send(which, visiting, step):
        if step == steps and block_count % 2 == 0:
            visiting = visiting[:half] if which == 0 else visiting[half:]
        return lax.ppermute(visiting, "blk", forward if which == 0 else backward)

    chains = [[payload, None, [payload]], [payload, None, []]]
    if steps >= 1:
        for which, chain in enumerate(chains):
            chain[0] = send(which, chain[0], 1)
            chain[2].append(chain[0])

    if group_count == 4:
        across = lax.ppermute(payload, "grp", partner_pairs(group_count, 2))
        beside = lax.ppermute(payload, "grp", partner_pairs(group_count, 1))
        diagonal = lax.ppermute(across, "grp", partner_pairs(group_count, 1))
        segment_pairs = [partner_pairs(group_count, k) for k in range(1, 4)]
        left_payload = jnp.concatenate([payload, beside, across, diagonal], axis=0)
    else:
        shifted = [lax.ppermute(payload, "grp", [(g, (g + k) % group_count) for g in range(group_count)])
                   for k in range(1, group_count)]
        segment_pairs = [[(g, (g - k) % group_count) for g in range(group_count)] for k in range(1, group_count)]
        left_payload = jnp.concatenate([payload] + shifted, axis=0)
    left_labels = tag_labels(left_payload)
    left_rows = left_payload[:, :D]

    def fold(best, blocks):
        for block in blocks:
            tile = block_best(left_rows, left_labels, block)
            best = tile if best is None else jnp.maximum(best, tile)
        return best

    for step in range(2, steps + 1):
        for which, chain in enumerate(chains):
            visiting, best, pending = chain
            visiting = send(which, visiting, step)
            best = fold(best, pending)
            visiting, best = lax.optimization_barrier((visiting, best))
            chain[0], chain[1], chain[2] = visiting, best, [visiting]
    best = None
    for _, chain_best, pending in chains:
        chain_best = fold(chain_best, pending)
        if chain_best is not None:
            best = chain_best if best is None else jnp.maximum(best, chain_best)

    best = best.reshape(group_count, rows_here)
    result = best[0]
    for k, pairs in enumerate(segment_pairs, start=1):
        result = jnp.maximum(result, lax.ppermute(best[k], "grp", pairs))
    return result


def solution(mesh):
    return jax.shard_map(
        per_device,
        mesh=mesh,
        in_specs=(P(("grp", "blk"), None), P(("grp", "blk")), P(("grp", "blk"))),
        out_specs=P(("grp", "blk")),
        check_vma=False,
    )
```

```python
import math

import jax
import jax.numpy as jnp
from jax import lax
from jax.sharding import PartitionSpec as P

D = 4096
TAG_WIDTH = 128
ORDER_SPAN = 8192.0


def ring_order(count):
    if count % 2:
        return list(range(count))
    return [2 * k for k in range(count // 2)] + [2 * k + 1 for k in reversed(range(count // 2))]


def tag_labels(payload):
    high = payload[:, D].astype(jnp.float32)
    low = payload[:, D + 1].astype(jnp.float32)
    return high * 128.0 + low


def block_best(left_rows, left_labels, payload):
    scores = jnp.einsum("id,jd->ij", left_rows, payload[:, :D], preferred_element_type=jnp.float32)
    right_labels = tag_labels(payload)
    same_cluster = jnp.floor(left_labels[:, None] / ORDER_SPAN) == jnp.floor(right_labels[None, :] / ORDER_SPAN)
    earlier = same_cluster & (right_labels[None, :] < left_labels[:, None])
    return jnp.max(jnp.where(earlier, scores, jnp.float32(-1.0)), axis=1)


def partner_pairs(group_count, mask):
    return [(g, g ^ mask) for g in range(group_count)]


def per_device(embeddings, cluster_ids, row_index):
    group_count = lax.axis_size("grp")
    block_count = lax.axis_size("blk")
    rows_here = embeddings.shape[0]
    widened = embeddings.astype(jnp.float32)
    square_sum = jnp.sum(widened * widened, axis=1, keepdims=True)
    scale = lax.rsqrt(square_sum / D + 1e-06)
    high = (cluster_ids * 64 + row_index // 128).astype(jnp.float32)[:, None]
    low = (row_index % 128).astype(jnp.float32)[:, None]
    column = jnp.arange(D + TAG_WIDTH)[None, :]
    padded = jnp.pad(embeddings, ((0, 0), (0, TAG_WIDTH))).astype(jnp.float32)
    tags = jnp.where(column == D, high, jnp.where(column == D + 1, low, 0.0))
    payload = jnp.where(column < D, padded * scale / math.sqrt(D), tags).astype(jnp.bfloat16)

    order = ring_order(block_count)
    forward = [(order[i], order[(i + 1) % block_count]) for i in range(block_count)]
    backward = [(dst, src) for src, dst in forward]
    half = rows_here // 2
    steps = block_count // 2
    lanes = [(0, 0), (0, 1), (1, 0), (1, 1)]

    def lane_steps(lane):
        which, part = lane
        if block_count % 2 == 0 and which != part:
            return steps - 1
        return steps

    def send(lane, visiting):
        which, _ = lane
        return lax.ppermute(visiting, "blk", forward if which == 0 else backward)

    chains = []
    for lane in lanes:
        piece = payload[:half] if lane[1] == 0 else payload[half:]
        chains.append([piece, None, [piece] if lane[0] == 0 else []])
    for lane, chain in zip(lanes, chains):
        if lane_steps(lane) >= 1:
            chain[0] = send(lane, chain[0])
            chain[2].append(chain[0])

    if group_count == 4:
        across = lax.ppermute(payload, "grp", partner_pairs(group_count, 2))
        beside = lax.ppermute(payload, "grp", partner_pairs(group_count, 1))
        diagonal = lax.ppermute(across, "grp", partner_pairs(group_count, 1))
        segment_pairs = [partner_pairs(group_count, k) for k in range(1, 4)]
        left_payload = jnp.concatenate([payload, beside, across, diagonal], axis=0)
    else:
        shifted = [lax.ppermute(payload, "grp", [(g, (g + k) % group_count) for g in range(group_count)])
                   for k in range(1, group_count)]
        segment_pairs = [[(g, (g - k) % group_count) for g in range(group_count)] for k in range(1, group_count)]
        left_payload = jnp.concatenate([payload] + shifted, axis=0)
    left_labels = tag_labels(left_payload)
    left_rows = left_payload[:, :D]

    def fold(best, blocks):
        for block in blocks:
            tile = block_best(left_rows, left_labels, block)
            best = tile if best is None else jnp.maximum(best, tile)
        return best

    for step in range(2, steps + 1):
        for lane, chain in zip(lanes, chains):
            if step > lane_steps(lane):
                continue
            visiting, best, pending = chain
            visiting = send(lane, visiting)
            best = fold(best, pending)
            visiting, best = lax.optimization_barrier((visiting, best))
            chain[0], chain[1], chain[2] = visiting, best, [visiting]
    best = None
    for chain_best, pending in [(c[1], c[2]) for c in chains]:
        chain_best = fold(chain_best, pending)
        if chain_best is not None:
            best = chain_best if best is None else jnp.maximum(best, chain_best)

    best = best.reshape(group_count, rows_here)
    result = best[0]
    for k, pairs in enumerate(segment_pairs, start=1):
        result = jnp.maximum(result, lax.ppermute(best[k], "grp", pairs))
    return result


def solution(mesh):
    return jax.shard_map(
        per_device,
        mesh=mesh,
        in_specs=(P(("grp", "blk"), None), P(("grp", "blk")), P(("grp", "blk"))),
        out_specs=P(("grp", "blk")),
        check_vma=False,
    )
```

```python
import math

import jax
import jax.numpy as jnp
from jax import lax
from jax.sharding import PartitionSpec as P

D = 4096
TAG_WIDTH = 128
ORDER_SPAN = 8192.0


def ring_order(count):
    if count % 2:
        return list(range(count))
    return [2 * k for k in range(count // 2)] + [2 * k + 1 for k in reversed(range(count // 2))]


def tag_labels(payload):
    high = payload[:, D].astype(jnp.float32)
    low = payload[:, D + 1].astype(jnp.float32)
    return high * 128.0 + low


def block_best(left_rows, left_labels, payload):
    scores = jnp.einsum("id,jd->ij", left_rows, payload[:, :D], preferred_element_type=jnp.float32)
    right_labels = tag_labels(payload)
    same_cluster = jnp.floor(left_labels[:, None] / ORDER_SPAN) == jnp.floor(right_labels[None, :] / ORDER_SPAN)
    earlier = same_cluster & (right_labels[None, :] < left_labels[:, None])
    return jnp.max(jnp.where(earlier, scores, jnp.float32(-1.0)), axis=1)


def partner_pairs(group_count, mask):
    return [(g, g ^ mask) for g in range(group_count)]


def per_device(embeddings, cluster_ids, row_index):
    group_count = lax.axis_size("grp")
    block_count = lax.axis_size("blk")
    rows_here = embeddings.shape[0]
    widened = embeddings.astype(jnp.float32)
    square_sum = jnp.sum(widened * widened, axis=1, keepdims=True)
    scale = lax.rsqrt(square_sum / D + 1e-06)
    high = (cluster_ids * 64 + row_index // 128).astype(jnp.float32)[:, None]
    low = (row_index % 128).astype(jnp.float32)[:, None]
    column = jnp.arange(D + TAG_WIDTH)[None, :]
    padded = jnp.pad(widened, ((0, 0), (0, TAG_WIDTH)))
    tags = jnp.where(column == D, high, jnp.where(column == D + 1, low, 0.0))
    payload = jnp.where(column < D, padded * scale / math.sqrt(D), tags).astype(jnp.bfloat16)

    order = ring_order(block_count)
    forward = [(order[i], order[(i + 1) % block_count]) for i in range(block_count)]
    backward = [(dst, src) for src, dst in forward]
    half = rows_here // 2
    steps = block_count // 2

    def send(which, visiting, step):
        if step == steps and block_count % 2 == 0:
            visiting = visiting[:half] if which == 0 else visiting[half:]
        return lax.ppermute(visiting, "blk", forward if which == 0 else backward)

    chains = [[payload, None, []], [payload, None, [payload]]]
    directions = [1, 0]
    if steps >= 1:
        for which, chain in zip(directions, chains):
            chain[0] = send(which, chain[0], 1)
            chain[2].append(chain[0])

    if group_count == 4:
        across = lax.ppermute(payload, "grp", partner_pairs(group_count, 2))
        beside = lax.ppermute(payload, "grp", partner_pairs(group_count, 1))
        diagonal = lax.ppermute(across, "grp", partner_pairs(group_count, 1))
        segment_pairs = [partner_pairs(group_count, k) for k in range(1, 4)]
        left_payload = jnp.concatenate([payload, beside, across, diagonal], axis=0)
    else:
        shifted = [lax.ppermute(payload, "grp", [(g, (g + k) % group_count) for g in range(group_count)])
                   for k in range(1, group_count)]
        segment_pairs = [[(g, (g - k) % group_count) for g in range(group_count)] for k in range(1, group_count)]
        left_payload = jnp.concatenate([payload] + shifted, axis=0)
    left_labels = tag_labels(left_payload)
    left_rows = left_payload[:, :D]

    def fold(best, blocks):
        for block in blocks:
            tile = block_best(left_rows, left_labels, block)
            best = tile if best is None else jnp.maximum(best, tile)
        return best

    for step in range(2, steps + 1):
        for which, chain in zip(directions, chains):
            visiting, best, pending = chain
            visiting = send(which, visiting, step)
            best = fold(best, pending)
            visiting, best = lax.optimization_barrier((visiting, best))
            chain[0], chain[1], chain[2] = visiting, best, [visiting]
    best = None
    for _, chain_best, pending in chains:
        chain_best = fold(chain_best, pending)
        if chain_best is not None:
            best = chain_best if best is None else jnp.maximum(best, chain_best)

    best = best.reshape(group_count, rows_here)
    result = best[0]
    for k, pairs in enumerate(segment_pairs, start=1):
        result = jnp.maximum(result, lax.ppermute(best[k], "grp", pairs))
    return result


def solution(mesh):
    return jax.shard_map(
        per_device,
        mesh=mesh,
        in_specs=(P(("grp", "blk"), None), P(("grp", "blk")), P(("grp", "blk"))),
        out_specs=P(("grp", "blk")),
        check_vma=False,
    )
```

```python
import math

import jax
import jax.numpy as jnp
from jax import lax
from jax.sharding import PartitionSpec as P

D = 4096
TAG_WIDTH = 128
ORDER_SPAN = 8192.0


def ring_order(count):
    if count % 2:
        return list(range(count))
    return [2 * k for k in range(count // 2)] + [2 * k + 1 for k in reversed(range(count // 2))]


def tag_labels(payload):
    high = payload[:, D].astype(jnp.float32)
    low = payload[:, D + 1].astype(jnp.float32)
    return high * 128.0 + low


def block_best(left_rows, left_labels, payload):
    scores = jnp.einsum("id,jd->ij", left_rows, payload[:, :D], preferred_element_type=jnp.float32)
    right_labels = tag_labels(payload)
    same_cluster = jnp.floor(left_labels[:, None] / ORDER_SPAN) == jnp.floor(right_labels[None, :] / ORDER_SPAN)
    earlier = same_cluster & (right_labels[None, :] < left_labels[:, None])
    return jnp.max(jnp.where(earlier, scores, jnp.float32(-1.0)), axis=1)


def partner_pairs(group_count, mask):
    return [(g, g ^ mask) for g in range(group_count)]


def per_device(embeddings, cluster_ids, row_index):
    group_count = lax.axis_size("grp")
    block_count = lax.axis_size("blk")
    rows_here = embeddings.shape[0]
    widened = embeddings.astype(jnp.float32)
    square_sum = jnp.sum(widened * widened, axis=1, keepdims=True)
    scale = lax.rsqrt(square_sum / D + 1e-06)
    high = (cluster_ids * 64 + row_index // 128).astype(jnp.float32)[:, None]
    low = (row_index % 128).astype(jnp.float32)[:, None]
    column = jnp.arange(D + TAG_WIDTH)[None, :]
    padded = jnp.pad(embeddings, ((0, 0), (0, TAG_WIDTH))).astype(jnp.float32)
    tags = jnp.where(column == D, high, jnp.where(column == D + 1, low, 0.0))
    payload = jnp.where(column < D, padded * scale / math.sqrt(D), tags).astype(jnp.bfloat16)

    order = ring_order(block_count)
    forward = [(order[i], order[(i + 1) % block_count]) for i in range(block_count)]
    backward = [(dst, src) for src, dst in forward]
    half = rows_here // 2
    steps = block_count // 2

    def send(which, visiting, step):
        if step == steps and block_count % 2 == 0:
            visiting = visiting[:half] if which == 0 else visiting[half:]
        return lax.ppermute(visiting, "blk", forward if which == 0 else backward)

    chains = [[payload, None, [payload]], [payload, None, []]]
    if steps >= 1:
        for which, chain in enumerate(chains):
            chain[0] = send(which, chain[0], 1)
            chain[2].append(chain[0])

    if group_count == 4:
        across = lax.ppermute(payload, "grp", partner_pairs(group_count, 2))
        beside = lax.ppermute(payload, "grp", partner_pairs(group_count, 1))
        diagonal = lax.ppermute(across, "grp", partner_pairs(group_count, 1))
        segment_pairs = [partner_pairs(group_count, k) for k in range(1, 4)]
        left_payload = jnp.concatenate([payload, beside, across, diagonal], axis=0)
    else:
        shifted = [lax.ppermute(payload, "grp", [(g, (g + k) % group_count) for g in range(group_count)])
                   for k in range(1, group_count)]
        segment_pairs = [[(g, (g - k) % group_count) for g in range(group_count)] for k in range(1, group_count)]
        left_payload = jnp.concatenate([payload] + shifted, axis=0)
    left_labels = tag_labels(left_payload)
    left_rows = left_payload[:, :D]

    def fold(best, blocks):
        for block in blocks:
            tile = block_best(left_rows, left_labels, block)
            best = tile if best is None else jnp.maximum(best, tile)
        return best

    for step in range(2, steps + 1):
        for which, chain in enumerate(chains):
            visiting, best, pending = chain
            visiting = send(which, visiting, step)
            best = fold(best, pending)
            visiting, best = lax.optimization_barrier((visiting, best))
            chain[0], chain[1], chain[2] = visiting, best, [visiting]
    best = None
    for _, chain_best, pending in chains:
        chain_best = fold(chain_best, pending)
        if chain_best is not None:
            best = chain_best if best is None else jnp.maximum(best, chain_best)

    best = best.reshape(group_count, rows_here)
    if group_count == 4:
        far = lax.ppermute(best[2:], "grp", partner_pairs(group_count, 2))
        near = jnp.maximum(best[:2], far)
        return jnp.maximum(near[0], lax.ppermute(near[1], "grp", partner_pairs(group_count, 1)))
    result = best[0]
    for k, pairs in enumerate(segment_pairs, start=1):
        result = jnp.maximum(result, lax.ppermute(best[k], "grp", pairs))
    return result


def solution(mesh):
    return jax.shard_map(
        per_device,
        mesh=mesh,
        in_specs=(P(("grp", "blk"), None), P(("grp", "blk")), P(("grp", "blk"))),
        out_specs=P(("grp", "blk")),
        check_vma=False,
    )
```

```python
import math

import jax
import jax.numpy as jnp
from jax import lax
from jax.sharding import PartitionSpec as P

D = 4096
TAG_WIDTH = 128
ORDER_SPAN = 8192.0


def ring_order(count):
    if count % 2:
        return list(range(count))
    return [2 * k for k in range(count // 2)] + [2 * k + 1 for k in reversed(range(count // 2))]


def tag_labels(payload):
    high = payload[:, D].astype(jnp.float32)
    low = payload[:, D + 1].astype(jnp.float32)
    return high * 128.0 + low


def block_best(left_rows, left_labels, payload):
    scores = jnp.einsum("id,jd->ij", left_rows, payload[:, :D], preferred_element_type=jnp.float32)
    right_labels = tag_labels(payload)
    same_cluster = jnp.floor(left_labels[:, None] / ORDER_SPAN) == jnp.floor(right_labels[None, :] / ORDER_SPAN)
    earlier = same_cluster & (right_labels[None, :] < left_labels[:, None])
    return jnp.max(jnp.where(earlier, scores, jnp.float32(-1.0)), axis=1)


def partner_pairs(group_count, mask):
    return [(g, g ^ mask) for g in range(group_count)]


def per_device(embeddings, cluster_ids, row_index):
    group_count = lax.axis_size("grp")
    block_count = lax.axis_size("blk")
    rows_here = embeddings.shape[0]
    widened = embeddings.astype(jnp.float32)
    square_sum = jnp.sum(widened * widened, axis=1, keepdims=True)
    scale = lax.rsqrt(square_sum / D + 1e-06)
    high = (cluster_ids * 64 + row_index // 128).astype(jnp.float32)[:, None]
    low = (row_index % 128).astype(jnp.float32)[:, None]
    column = jnp.arange(D + TAG_WIDTH)[None, :]
    padded = jnp.pad(widened, ((0, 0), (0, TAG_WIDTH)))
    tags = jnp.where(column == D, high, jnp.where(column == D + 1, low, 0.0))
    payload = jnp.where(column < D, padded * scale / math.sqrt(D), tags).astype(jnp.bfloat16)

    order = ring_order(block_count)
    forward = [(order[i], order[(i + 1) % block_count]) for i in range(block_count)]
    backward = [(dst, src) for src, dst in forward]
    split = min(rows_here, max(0, (rows_here * 5 // 8) // 8 * 8))
    steps = block_count // 2

    def send(which, visiting, step):
        if step == steps and block_count % 2 == 0:
            visiting = visiting[:split] if which == 0 else visiting[split:]
        return lax.ppermute(visiting, "blk", forward if which == 0 else backward)

    chains = [[payload, None, [payload]], [payload, None, []]]
    if steps >= 1:
        for which, chain in enumerate(chains):
            chain[0] = send(which, chain[0], 1)
            chain[2].append(chain[0])

    if group_count == 4:
        across = lax.ppermute(payload, "grp", partner_pairs(group_count, 2))
        beside = lax.ppermute(payload, "grp", partner_pairs(group_count, 1))
        diagonal = lax.ppermute(across, "grp", partner_pairs(group_count, 1))
        segment_pairs = [partner_pairs(group_count, k) for k in range(1, 4)]
        left_payload = jnp.concatenate([payload, beside, across, diagonal], axis=0)
    else:
        shifted = [lax.ppermute(payload, "grp", [(g, (g + k) % group_count) for g in range(group_count)])
                   for k in range(1, group_count)]
        segment_pairs = [[(g, (g - k) % group_count) for g in range(group_count)] for k in range(1, group_count)]
        left_payload = jnp.concatenate([payload] + shifted, axis=0)
    left_labels = tag_labels(left_payload)
    left_rows = left_payload[:, :D]

    def fold(best, blocks):
        for block in blocks:
            tile = block_best(left_rows, left_labels, block)
            best = tile if best is None else jnp.maximum(best, tile)
        return best

    for step in range(2, steps + 1):
        for which, chain in enumerate(chains):
            visiting, best, pending = chain
            visiting = send(which, visiting, step)
            best = fold(best, pending)
            visiting, best = lax.optimization_barrier((visiting, best))
            chain[0], chain[1], chain[2] = visiting, best, [visiting]
    best = None
    for _, chain_best, pending in chains:
        chain_best = fold(chain_best, pending)
        if chain_best is not None:
            best = chain_best if best is None else jnp.maximum(best, chain_best)

    best = best.reshape(group_count, rows_here)
    result = best[0]
    for k, pairs in enumerate(segment_pairs, start=1):
        result = jnp.maximum(result, lax.ppermute(best[k], "grp", pairs))
    return result


def solution(mesh):
    return jax.shard_map(
        per_device,
        mesh=mesh,
        in_specs=(P(("grp", "blk"), None), P(("grp", "blk")), P(("grp", "blk"))),
        out_specs=P(("grp", "blk")),
        check_vma=False,
    )
```

```python
import math

import jax
import jax.numpy as jnp
from jax import lax
from jax.sharding import PartitionSpec as P

D = 4096
TAG_WIDTH = 128
ORDER_SPAN = 8192.0


def tag_labels(payload):
    high = payload[:, D].astype(jnp.float32)
    low = payload[:, D + 1].astype(jnp.float32)
    return high * 128.0 + low


def block_best(left_rows, left_labels, payload):
    scores = jnp.einsum("id,jd->ij", left_rows, payload[:, :D], preferred_element_type=jnp.float32)
    right_labels = tag_labels(payload)
    same_cluster = jnp.floor(left_labels[:, None] / ORDER_SPAN) == jnp.floor(right_labels[None, :] / ORDER_SPAN)
    earlier = same_cluster & (right_labels[None, :] < left_labels[:, None])
    return jnp.max(jnp.where(earlier, scores, jnp.float32(-1.0)), axis=1)


def per_device(embeddings, cluster_ids, row_index):
    group_count = lax.axis_size("grp")
    block_count = lax.axis_size("blk")
    rows_here = embeddings.shape[0]
    widened = embeddings.astype(jnp.float32)
    square_sum = jnp.sum(widened * widened, axis=1, keepdims=True)
    scale = lax.rsqrt(square_sum / D + 1e-06)
    high = (cluster_ids * 64 + row_index // 128).astype(jnp.float32)[:, None]
    low = (row_index % 128).astype(jnp.float32)[:, None]
    column = jnp.arange(D + TAG_WIDTH)[None, :]
    padded = jnp.pad(widened, ((0, 0), (0, TAG_WIDTH)))
    tags = jnp.where(column == D, high, jnp.where(column == D + 1, low, 0.0))
    payload = jnp.where(column < D, padded * scale / math.sqrt(D), tags).astype(jnp.bfloat16)

    lo = 2 if block_count % 2 == 0 else 1
    line_count = block_count // lo
    mesh_axes = ("grp", "blk")

    def xor_pairs(dg, dl):
        return [(g * block_count + b, (g ^ dg) * block_count + (b ^ dl))
                for g in range(group_count) for b in range(block_count)]

    def line_pairs(step, up):
        pairs = []
        for part in range(lo):
            for h in range(line_count):
                if up and step - 1 <= h <= line_count - 2:
                    pairs.append((h * lo + part, (h + 1) * lo + part))
                if not up and 1 <= h <= line_count - step:
                    pairs.append((h * lo + part, (h - 1) * lo + part))
        return pairs

    chains = [[payload, None, [], True], [payload, None, [], False]]
    line_steps = line_count - 1
    my_line = lax.axis_index("blk") // lo
    if line_steps >= 1:
        for chain in chains:
            chain[0] = lax.ppermute(chain[0], "blk", line_pairs(1, chain[3]))
            chain[2].append((chain[0], 1))

    if group_count == 4 and lo == 2:
        half = rows_here // 2
        beside_x = lax.ppermute(payload, "blk", [(b, b ^ 1) for b in range(block_count)])
        beside_y = lax.ppermute(payload, "grp", [(g, g ^ 2) for g in range(group_count)])
        far_top = lax.ppermute(beside_x[:half], "grp", [(g, g ^ 2) for g in range(group_count)])
        far_bottom = lax.ppermute(beside_y[half:], "blk", [(b, b ^ 1) for b in range(block_count)])
        far = jnp.concatenate([far_top, far_bottom], axis=0)
        same_core = [payload, beside_x, beside_y, far]
        other_core = [lax.ppermute(block, "grp", [(g, g ^ 1) for g in range(group_count)]) for block in same_core]
        offsets = [(0, 0), (0, 1), (2, 0), (2, 1), (1, 0), (1, 1), (3, 0), (3, 1)]
        left_payload = jnp.concatenate(same_core + other_core, axis=0)
    else:
        offsets = [(dg, dl) for dg in range(group_count) for dl in range(lo)]
        blocks = []
        for dg, dl in offsets:
            if dg == 0 and dl == 0:
                blocks.append(payload)
            else:
                pairs = [(((g + dg) % group_count) * block_count + (b ^ dl), g * block_count + b)
                         for g in range(group_count) for b in range(block_count)]
                blocks.append(lax.ppermute(payload, mesh_axes, pairs))
        left_payload = jnp.concatenate(blocks, axis=0)
    left_labels = tag_labels(left_payload)
    left_rows = left_payload[:, :D]

    def fold(best, blocks, up):
        for block, step in blocks:
            tile = block_best(left_rows, left_labels, block)
            if step:
                valid = my_line >= step if up else my_line + step <= line_count - 1
                tile = jnp.where(valid, tile, jnp.float32(-1.0))
            best = tile if best is None else jnp.maximum(best, tile)
        return best

    best = block_best(left_rows, left_labels, payload)
    for step in range(2, line_steps + 1):
        for chain in chains:
            visiting, chain_best, pending, up = chain
            visiting = lax.ppermute(visiting, "blk", line_pairs(step, up))
            chain_best = fold(chain_best, pending, up)
            visiting, chain_best = lax.optimization_barrier((visiting, chain_best))
            chain[0], chain[1], chain[2] = visiting, chain_best, [(visiting, step)]
    for visiting, chain_best, pending, up in chains:
        chain_best = fold(chain_best, pending, up)
        if chain_best is not None:
            best = jnp.maximum(best, chain_best)

    best = best.reshape(len(offsets), rows_here)
    result = best[0]
    for k in range(1, len(offsets)):
        dg, dl = offsets[k]
        if group_count == 4 and lo == 2:
            pairs = xor_pairs(dg, dl)
        else:
            pairs = [(g * block_count + b, ((g + dg) % group_count) * block_count + (b ^ dl))
                     for g in range(group_count) for b in range(block_count)]
        result = jnp.maximum(result, lax.ppermute(best[k], mesh_axes, pairs))
    return result


def solution(mesh):
    return jax.shard_map(
        per_device,
        mesh=mesh,
        in_specs=(P(("grp", "blk"), None), P(("grp", "blk")), P(("grp", "blk"))),
        out_specs=P(("grp", "blk")),
        check_vma=False,
    )
```

```python
import math

import jax
import jax.numpy as jnp
from jax import lax
from jax.sharding import PartitionSpec as P

D = 4096
TAG_WIDTH = 128
ORDER_SPAN = 8192.0


def ring_order(count):
    if count % 2:
        return list(range(count))
    return [2 * k for k in range(count // 2)] + [2 * k + 1 for k in reversed(range(count // 2))]


def tag_labels(payload):
    high = payload[:, D].astype(jnp.float32)
    low = payload[:, D + 1].astype(jnp.float32)
    return high * 128.0 + low


def block_best(left_rows, left_labels, payload):
    scores = jnp.einsum("id,jd->ij", left_rows, payload[:, :D], preferred_element_type=jnp.float32)
    right_labels = tag_labels(payload)
    same_cluster = jnp.floor(left_labels[:, None] / ORDER_SPAN) == jnp.floor(right_labels[None, :] / ORDER_SPAN)
    earlier = same_cluster & (right_labels[None, :] < left_labels[:, None])
    return jnp.max(jnp.where(earlier, scores, jnp.float32(-1.0)), axis=1)


def partner_pairs(group_count, mask):
    return [(g, g ^ mask) for g in range(group_count)]


def per_device(embeddings, cluster_ids, row_index):
    group_count = lax.axis_size("grp")
    block_count = lax.axis_size("blk")
    rows_here = embeddings.shape[0]
    widened = embeddings.astype(jnp.float32)
    square_sum = jnp.sum(widened * widened, axis=1, keepdims=True)
    scale = lax.rsqrt(square_sum / D + 1e-06)
    high = (cluster_ids * 64 + row_index // 128).astype(jnp.float32)[:, None]
    low = (row_index % 128).astype(jnp.float32)[:, None]
    column = jnp.arange(D + TAG_WIDTH)[None, :]
    padded = jnp.pad(widened, ((0, 0), (0, TAG_WIDTH)))
    tags = jnp.where(column == D, high, jnp.where(column == D + 1, low, 0.0))
    payload = jnp.where(column < D, padded * scale / math.sqrt(D), tags).astype(jnp.bfloat16)

    order = ring_order(block_count)
    forward = [(order[i], order[(i + 1) % block_count]) for i in range(block_count)]
    backward = [(dst, src) for src, dst in forward]
    half = rows_here // 2
    steps = block_count // 2

    def send(which, visiting, step):
        if step == steps and block_count % 2 == 0:
            visiting = visiting[:half] if which == 0 else visiting[half:]
        return lax.ppermute(visiting, "blk", forward if which == 0 else backward)

    chains = [[payload, None, [payload]], [payload, None, []]]
    if steps >= 1:
        for which, chain in enumerate(chains):
            chain[0] = send(which, chain[0], 1)
            chain[2].append(chain[0])

    if group_count == 4:
        across = lax.ppermute(payload, "grp", partner_pairs(group_count, 2))
        beside = lax.ppermute(payload, "grp", partner_pairs(group_count, 1))
        diagonal = lax.ppermute(across, "grp", partner_pairs(group_count, 1))
        segment_pairs = [partner_pairs(group_count, k) for k in range(1, 4)]
        left_payload = jnp.concatenate([payload, beside, across, diagonal], axis=0)
    else:
        shifted = [lax.ppermute(payload, "grp", [(g, (g + k) % group_count) for g in range(group_count)])
                   for k in range(1, group_count)]
        segment_pairs = [[(g, (g - k) % group_count) for g in range(group_count)] for k in range(1, group_count)]
        left_payload = jnp.concatenate([payload] + shifted, axis=0)
    left_labels = tag_labels(left_payload)
    left_rows = left_payload[:, :D]

    def fold(best, blocks):
        for block in blocks:
            tile = block_best(left_rows, left_labels, block)
            best = tile if best is None else jnp.maximum(best, tile)
        return best

    for step in range(2, steps + 1):
        for which, chain in enumerate(chains):
            visiting, best, pending = chain
            visiting = send(which, visiting, step)
            best = fold(best, pending)
            chain[0], chain[1], chain[2] = visiting, best, [visiting]
    best = None
    for _, chain_best, pending in chains:
        chain_best = fold(chain_best, pending)
        if chain_best is not None:
            best = chain_best if best is None else jnp.maximum(best, chain_best)

    best = best.reshape(group_count, rows_here)
    result = best[0]
    for k, pairs in enumerate(segment_pairs, start=1):
        result = jnp.maximum(result, lax.ppermute(best[k], "grp", pairs))
    return result


def solution(mesh):
    return jax.shard_map(
        per_device,
        mesh=mesh,
        in_specs=(P(("grp", "blk"), None), P(("grp", "blk")), P(("grp", "blk"))),
        out_specs=P(("grp", "blk")),
        check_vma=False,
    )
```

```python
import math

import jax
import jax.numpy as jnp
from jax import lax
from jax.sharding import PartitionSpec as P

D = 4096
TAG_WIDTH = 128
ORDER_SPAN = 8192.0


def ring_order(count):
    if count % 2:
        return list(range(count))
    return [2 * k for k in range(count // 2)] + [2 * k + 1 for k in reversed(range(count // 2))]


def tag_labels(payload):
    high = payload[:, D].astype(jnp.float32)
    low = payload[:, D + 1].astype(jnp.float32)
    return high * 128.0 + low


def block_best(left_rows, left_labels, payload):
    scores = jnp.einsum("id,jd->ij", left_rows, payload[:, :D], preferred_element_type=jnp.float32)
    right_labels = tag_labels(payload)
    same_cluster = jnp.floor(left_labels[:, None] / ORDER_SPAN) == jnp.floor(right_labels[None, :] / ORDER_SPAN)
    earlier = same_cluster & (right_labels[None, :] < left_labels[:, None])
    return jnp.max(jnp.where(earlier, scores, jnp.float32(-1.0)), axis=1)


def partner_pairs(group_count, mask):
    return [(g, g ^ mask) for g in range(group_count)]


def per_device(embeddings, cluster_ids, row_index):
    group_count = lax.axis_size("grp")
    block_count = lax.axis_size("blk")
    rows_here = embeddings.shape[0]
    widened = embeddings.astype(jnp.float32)
    square_sum = jnp.sum(widened * widened, axis=1, keepdims=True)
    scale = lax.rsqrt(square_sum / D + 1e-06)
    high = (cluster_ids * 64 + row_index // 128).astype(jnp.float32)[:, None]
    low = (row_index % 128).astype(jnp.float32)[:, None]
    column = jnp.arange(D + TAG_WIDTH)[None, :]
    padded = jnp.pad(widened, ((0, 0), (0, TAG_WIDTH)))
    tags = jnp.where(column == D, high, jnp.where(column == D + 1, low, 0.0))
    payload = jnp.where(column < D, padded * scale / math.sqrt(D), tags).astype(jnp.bfloat16)

    order = ring_order(block_count)
    forward = [(order[i], order[(i + 1) % block_count]) for i in range(block_count)]
    backward = [(dst, src) for src, dst in forward]
    half = rows_here // 2
    steps = block_count // 2

    def send(which, visiting, step):
        if step == steps and block_count % 2 == 0:
            visiting = visiting[:half] if which == 0 else visiting[half:]
        return lax.ppermute(visiting, "blk", forward if which == 0 else backward)

    chains = [[payload, None, [payload]], [payload, None, []]]
    if steps >= 1:
        for which, chain in enumerate(chains):
            chain[0] = send(which, chain[0], 1)
            chain[2].append(chain[0])

    if group_count == 4:
        across = lax.ppermute(payload, "grp", partner_pairs(group_count, 2))
        beside = lax.ppermute(payload, "grp", partner_pairs(group_count, 1))
        diagonal = lax.ppermute(across, "grp", partner_pairs(group_count, 1))
        segment_pairs = [partner_pairs(group_count, k) for k in range(1, 4)]
        left_payload = jnp.concatenate([payload, beside, across, diagonal], axis=0)
    else:
        shifted = [lax.ppermute(payload, "grp", [(g, (g + k) % group_count) for g in range(group_count)])
                   for k in range(1, group_count)]
        segment_pairs = [[(g, (g - k) % group_count) for g in range(group_count)] for k in range(1, group_count)]
        left_payload = jnp.concatenate([payload] + shifted, axis=0)
    left_labels = tag_labels(left_payload)
    left_rows = left_payload[:, :D]

    def fold(best, blocks):
        for block in blocks:
            tile = block_best(left_rows, left_labels, block)
            best = tile if best is None else jnp.maximum(best, tile)
        return best

    for step in range(2, steps + 1):
        for which, chain in enumerate(chains):
            visiting, best, pending = chain
            visiting = send(which, visiting, step)
            best = fold(best, pending)
            chain[0], chain[1], chain[2] = visiting, best, [visiting]
    if steps >= 1 and block_count % 2 == 0:
        chains[0][2] = [jnp.concatenate([chains[0][2][-1], chains[1][2][-1]], axis=0)] + chains[0][2][:-1]
        chains[1][2] = chains[1][2][:-1]
    best = None
    for _, chain_best, pending in chains:
        chain_best = fold(chain_best, pending)
        if chain_best is not None:
            best = chain_best if best is None else jnp.maximum(best, chain_best)

    best = best.reshape(group_count, rows_here)
    result = best[0]
    for k, pairs in enumerate(segment_pairs, start=1):
        result = jnp.maximum(result, lax.ppermute(best[k], "grp", pairs))
    return result


def solution(mesh):
    return jax.shard_map(
        per_device,
        mesh=mesh,
        in_specs=(P(("grp", "blk"), None), P(("grp", "blk")), P(("grp", "blk"))),
        out_specs=P(("grp", "blk")),
        check_vma=False,
    )
```

```python
import math

import jax
import jax.numpy as jnp
from jax import lax
from jax.sharding import PartitionSpec as P

D = 4096
TAG_WIDTH = 128
ORDER_SPAN = 8192.0


def ring_order(count):
    if count % 2:
        return list(range(count))
    return [2 * k for k in range(count // 2)] + [2 * k + 1 for k in reversed(range(count // 2))]


def tag_labels(payload):
    high = payload[:, D].astype(jnp.float32)
    low = payload[:, D + 1].astype(jnp.float32)
    return high * 128.0 + low


def block_best(left_rows, left_labels, payload):
    scores = jnp.einsum("id,jd->ij", left_rows, payload[:, :D], preferred_element_type=jnp.float32)
    right_labels = tag_labels(payload)
    same_cluster = jnp.floor(left_labels[:, None] / ORDER_SPAN) == jnp.floor(right_labels[None, :] / ORDER_SPAN)
    earlier = same_cluster & (right_labels[None, :] < left_labels[:, None])
    return jnp.max(jnp.where(earlier, scores, jnp.float32(-1.0)), axis=1)


def partner_pairs(group_count, mask):
    return [(g, g ^ mask) for g in range(group_count)]


def per_device(embeddings, cluster_ids, row_index):
    group_count = lax.axis_size("grp")
    block_count = lax.axis_size("blk")
    rows_here = embeddings.shape[0]
    widened = embeddings.astype(jnp.float32)
    squares = (widened * widened).reshape(rows_here, -1, 128)
    partial_sums = lax.optimization_barrier(jnp.sum(squares, axis=1))
    square_sum = jnp.sum(partial_sums, axis=1, keepdims=True)
    scale = lax.rsqrt(square_sum / D + 1e-06)
    high = (cluster_ids * 64 + row_index // 128).astype(jnp.float32)[:, None]
    low = (row_index % 128).astype(jnp.float32)[:, None]
    column = jnp.arange(D + TAG_WIDTH)[None, :]
    padded = jnp.pad(widened, ((0, 0), (0, TAG_WIDTH)))
    tags = jnp.where(column == D, high, jnp.where(column == D + 1, low, 0.0))
    payload = jnp.where(column < D, padded * scale / math.sqrt(D), tags).astype(jnp.bfloat16)

    order = ring_order(block_count)
    forward = [(order[i], order[(i + 1) % block_count]) for i in range(block_count)]
    backward = [(dst, src) for src, dst in forward]
    half = rows_here // 2
    steps = block_count // 2

    def send(which, visiting, step):
        if step == steps and block_count % 2 == 0:
            visiting = visiting[:half] if which == 0 else visiting[half:]
        return lax.ppermute(visiting, "blk", forward if which == 0 else backward)

    chains = [[payload, None, [payload]], [payload, None, []]]
    if steps >= 1:
        for which, chain in enumerate(chains):
            chain[0] = send(which, chain[0], 1)
            chain[2].append(chain[0])

    if group_count == 4:
        across = lax.ppermute(payload, "grp", partner_pairs(group_count, 2))
        beside = lax.ppermute(payload, "grp", partner_pairs(group_count, 1))
        diagonal = lax.ppermute(across, "grp", partner_pairs(group_count, 1))
        segment_pairs = [partner_pairs(group_count, k) for k in range(1, 4)]
        left_payload = jnp.concatenate([payload, beside, across, diagonal], axis=0)
    else:
        shifted = [lax.ppermute(payload, "grp", [(g, (g + k) % group_count) for g in range(group_count)])
                   for k in range(1, group_count)]
        segment_pairs = [[(g, (g - k) % group_count) for g in range(group_count)] for k in range(1, group_count)]
        left_payload = jnp.concatenate([payload] + shifted, axis=0)
    left_labels = tag_labels(left_payload)
    left_rows = left_payload[:, :D]

    def fold(best, blocks):
        for block in blocks:
            tile = block_best(left_rows, left_labels, block)
            best = tile if best is None else jnp.maximum(best, tile)
        return best

    for step in range(2, steps + 1):
        for which, chain in enumerate(chains):
            visiting, best, pending = chain
            visiting = send(which, visiting, step)
            best = fold(best, pending)
            chain[0], chain[1], chain[2] = visiting, best, [visiting]
    if steps >= 1 and block_count % 2 == 0:
        chains[0][2] = [jnp.concatenate([chains[0][2][-1], chains[1][2][-1]], axis=0)] + chains[0][2][:-1]
        chains[1][2] = chains[1][2][:-1]
    best = None
    for _, chain_best, pending in chains:
        chain_best = fold(chain_best, pending)
        if chain_best is not None:
            best = chain_best if best is None else jnp.maximum(best, chain_best)

    best = best.reshape(group_count, rows_here)
    result = best[0]
    for k, pairs in enumerate(segment_pairs, start=1):
        result = jnp.maximum(result, lax.ppermute(best[k], "grp", pairs))
    return result


def solution(mesh):
    return jax.shard_map(
        per_device,
        mesh=mesh,
        in_specs=(P(("grp", "blk"), None), P(("grp", "blk")), P(("grp", "blk"))),
        out_specs=P(("grp", "blk")),
        check_vma=False,
    )
```

```python
import math

import jax
import jax.numpy as jnp
from jax import lax
from jax.sharding import PartitionSpec as P

D = 4096
TAG_WIDTH = 128
ORDER_SPAN = 8192.0


def ring_order(count):
    if count % 2:
        return list(range(count))
    return [2 * k for k in range(count // 2)] + [2 * k + 1 for k in reversed(range(count // 2))]


def tag_labels(payload):
    high = payload[:, D].astype(jnp.float32)
    low = payload[:, D + 1].astype(jnp.float32)
    return high * 128.0 + low


def block_best(left_rows, left_labels, payload):
    scores = jnp.einsum("id,jd->ij", left_rows, payload[:, :D], preferred_element_type=jnp.float32)
    right_labels = tag_labels(payload)
    same_cluster = jnp.floor(left_labels[:, None] / ORDER_SPAN) == jnp.floor(right_labels[None, :] / ORDER_SPAN)
    earlier = same_cluster & (right_labels[None, :] < left_labels[:, None])
    return jnp.max(jnp.where(earlier, scores, jnp.float32(-1.0)), axis=1)


def partner_pairs(group_count, mask):
    return [(g, g ^ mask) for g in range(group_count)]


def per_device(embeddings, cluster_ids, row_index):
    group_count = lax.axis_size("grp")
    block_count = lax.axis_size("blk")
    rows_here = embeddings.shape[0]
    widened = embeddings.astype(jnp.float32)
    square_sum = jnp.sum(widened * widened, axis=1, keepdims=True)
    scale = lax.rsqrt(square_sum / D + 1e-06)
    high = (cluster_ids * 64 + row_index // 128).astype(jnp.float32)[:, None]
    low = (row_index % 128).astype(jnp.float32)[:, None]
    column = jnp.arange(D + TAG_WIDTH)[None, :]
    padded = jnp.pad(widened, ((0, 0), (0, TAG_WIDTH)))
    tags = jnp.where(column == D, high, jnp.where(column == D + 1, low, 0.0))
    payload = jnp.where(column < D, padded * scale / math.sqrt(D), tags).astype(jnp.bfloat16)

    order = ring_order(block_count)
    forward = [(order[i], order[(i + 1) % block_count]) for i in range(block_count)]
    backward = [(dst, src) for src, dst in forward]
    half = rows_here // 2
    steps = block_count // 2

    def send(which, visiting, step):
        if step == steps and block_count % 2 == 0:
            visiting = visiting[:half] if which == 0 else visiting[half:]
        return lax.ppermute(visiting, "blk", forward if which == 0 else backward)

    chains = [[payload, None, [payload]], [payload, None, []]]
    if steps >= 1:
        for which, chain in enumerate(chains):
            chain[0] = send(which, chain[0], 1)
            chain[2].append(chain[0])

    if group_count == 4:
        later = payload
        if steps >= 1:
            later, _ = lax.optimization_barrier((payload, chains[0][0]))
        across = lax.ppermute(later, "grp", partner_pairs(group_count, 2))
        beside = lax.ppermute(payload, "grp", partner_pairs(group_count, 1))
        diagonal = lax.ppermute(across, "grp", partner_pairs(group_count, 1))
        segment_pairs = [partner_pairs(group_count, k) for k in range(1, 4)]
        left_payload = jnp.concatenate([payload, beside, across, diagonal], axis=0)
    else:
        shifted = [lax.ppermute(payload, "grp", [(g, (g + k) % group_count) for g in range(group_count)])
                   for k in range(1, group_count)]
        segment_pairs = [[(g, (g - k) % group_count) for g in range(group_count)] for k in range(1, group_count)]
        left_payload = jnp.concatenate([payload] + shifted, axis=0)
    left_labels = tag_labels(left_payload)
    left_rows = left_payload[:, :D]

    def fold(best, blocks):
        for block in blocks:
            tile = block_best(left_rows, left_labels, block)
            best = tile if best is None else jnp.maximum(best, tile)
        return best

    for step in range(2, steps + 1):
        for which, chain in enumerate(chains):
            visiting, best, pending = chain
            visiting = send(which, visiting, step)
            best = fold(best, pending)
            if step >= 3:
                visiting, best = lax.optimization_barrier((visiting, best))
            chain[0], chain[1], chain[2] = visiting, best, [visiting]
    if steps >= 1 and block_count % 2 == 0:
        chains[0][2] = [jnp.concatenate([chains[0][2][-1], chains[1][2][-1]], axis=0)] + chains[0][2][:-1]
        chains[1][2] = chains[1][2][:-1]
    best = None
    for _, chain_best, pending in chains:
        chain_best = fold(chain_best, pending)
        if chain_best is not None:
            best = chain_best if best is None else jnp.maximum(best, chain_best)

    best = best.reshape(group_count, rows_here)
    result = best[0]
    for k, pairs in enumerate(segment_pairs, start=1):
        result = jnp.maximum(result, lax.ppermute(best[k], "grp", pairs))
    return result


def solution(mesh):
    return jax.shard_map(
        per_device,
        mesh=mesh,
        in_specs=(P(("grp", "blk"), None), P(("grp", "blk")), P(("grp", "blk"))),
        out_specs=P(("grp", "blk")),
        check_vma=False,
    )
```

```python
import math

import jax
import jax.numpy as jnp
from jax import lax
from jax.experimental import pallas as pl
from jax.experimental.pallas import tpu as pltpu
from jax.sharding import PartitionSpec as P

D = 4096
TAG_WIDTH = 128
ORDER_SPAN = 8192.0


def ring_order(count):
    if count % 2:
        return list(range(count))
    return [2 * k for k in range(count // 2)] + [2 * k + 1 for k in reversed(range(count // 2))]


def tag_labels(payload):
    high = payload[:, D].astype(jnp.float32)
    low = payload[:, D + 1].astype(jnp.float32)
    return high * 128.0 + low


def block_best(left_rows, left_labels, payload):
    scores = jnp.einsum("id,jd->ij", left_rows, payload[:, :D], preferred_element_type=jnp.float32)
    right_labels = tag_labels(payload)
    same_cluster = jnp.floor(left_labels[:, None] / ORDER_SPAN) == jnp.floor(right_labels[None, :] / ORDER_SPAN)
    earlier = same_cluster & (right_labels[None, :] < left_labels[:, None])
    return jnp.max(jnp.where(earlier, scores, jnp.float32(-1.0)), axis=1)


def payload_kernel(rows_ref, cluster_ref, index_ref, out_ref):
    widened = rows_ref[...].astype(jnp.float32)
    square_sum = jnp.sum(widened * widened, axis=1, keepdims=True)
    scale = lax.rsqrt(square_sum / D + 1e-06)
    out_ref[:, :D] = (widened * scale / math.sqrt(D)).astype(jnp.bfloat16)
    index = index_ref[...]
    high = (cluster_ref[...] * 64 + index // 128).astype(jnp.float32)
    low = (index % 128).astype(jnp.float32)
    column = lax.broadcasted_iota(jnp.int32, (out_ref.shape[0], TAG_WIDTH), 1)
    tags = jnp.where(column == 0, high, jnp.where(column == 1, low, 0.0))
    out_ref[:, D:] = tags.astype(jnp.bfloat16)


def build_payload(embeddings, cluster_ids, row_index):
    rows = embeddings.shape[0]
    return pl.pallas_call(
        payload_kernel,
        out_shape=jax.ShapeDtypeStruct((rows, D + TAG_WIDTH), jnp.bfloat16),
        in_specs=[pl.BlockSpec(memory_space=pltpu.VMEM)] * 3,
        out_specs=pl.BlockSpec(memory_space=pltpu.VMEM),
        cost_estimate=pl.CostEstimate(flops=4 * rows * D, bytes_accessed=4 * rows * D + 2 * rows * TAG_WIDTH,
                                      transcendentals=rows),
    )(embeddings, cluster_ids.reshape(rows, 1), row_index.reshape(rows, 1))


def partner_pairs(group_count, mask):
    return [(g, g ^ mask) for g in range(group_count)]


def per_device(embeddings, cluster_ids, row_index):
    group_count = lax.axis_size("grp")
    block_count = lax.axis_size("blk")
    rows_here = embeddings.shape[0]
    payload = build_payload(embeddings, cluster_ids, row_index)

    order = ring_order(block_count)
    forward = [(order[i], order[(i + 1) % block_count]) for i in range(block_count)]
    backward = [(dst, src) for src, dst in forward]
    half = rows_here // 2
    steps = block_count // 2

    def send(which, visiting, step):
        if step == steps and block_count % 2 == 0:
            visiting = visiting[:half] if which == 0 else visiting[half:]
        return lax.ppermute(visiting, "blk", forward if which == 0 else backward)

    chains = [[payload, None, [payload]], [payload, None, []]]
    if steps >= 1:
        for which, chain in enumerate(chains):
            chain[0] = send(which, chain[0], 1)
            chain[2].append(chain[0])

    if group_count == 4:
        across = lax.ppermute(payload, "grp", partner_pairs(group_count, 2))
        beside = lax.ppermute(payload, "grp", partner_pairs(group_count, 1))
        diagonal = lax.ppermute(across, "grp", partner_pairs(group_count, 1))
        segment_pairs = [partner_pairs(group_count, k) for k in range(1, 4)]
        left_payload = jnp.concatenate([payload, beside, across, diagonal], axis=0)
    else:
        shifted = [lax.ppermute(payload, "grp", [(g, (g + k) % group_count) for g in range(group_count)])
                   for k in range(1, group_count)]
        segment_pairs = [[(g, (g - k) % group_count) for g in range(group_count)] for k in range(1, group_count)]
        left_payload = jnp.concatenate([payload] + shifted, axis=0)
    left_labels = tag_labels(left_payload)
    left_rows = left_payload[:, :D]

    def fold(best, blocks):
        for block in blocks:
            tile = block_best(left_rows, left_labels, block)
            best = tile if best is None else jnp.maximum(best, tile)
        return best

    for step in range(2, steps + 1):
        for which, chain in enumerate(chains):
            visiting, best, pending = chain
            visiting = send(which, visiting, step)
            best = fold(best, pending)
            chain[0], chain[1], chain[2] = visiting, best, [visiting]
    if steps >= 1 and block_count % 2 == 0:
        chains[0][2] = [jnp.concatenate([chains[0][2][-1], chains[1][2][-1]], axis=0)] + chains[0][2][:-1]
        chains[1][2] = chains[1][2][:-1]
    best = None
    for _, chain_best, pending in chains:
        chain_best = fold(chain_best, pending)
        if chain_best is not None:
            best = chain_best if best is None else jnp.maximum(best, chain_best)

    best = best.reshape(group_count, rows_here)
    result = best[0]
    for k, pairs in enumerate(segment_pairs, start=1):
        result = jnp.maximum(result, lax.ppermute(best[k], "grp", pairs))
    return result


def solution(mesh):
    return jax.shard_map(
        per_device,
        mesh=mesh,
        in_specs=(P(("grp", "blk"), None), P(("grp", "blk")), P(("grp", "blk"))),
        out_specs=P(("grp", "blk")),
        check_vma=False,
    )
```

```python
import math

import jax
import jax.numpy as jnp
from jax import lax
from jax.sharding import PartitionSpec as P

D = 4096
TAG_WIDTH = 128
ORDER_SPAN = 8192.0


def ring_order(count):
    if count % 2:
        return list(range(count))
    return [2 * k for k in range(count // 2)] + [2 * k + 1 for k in reversed(range(count // 2))]


def tag_labels(payload):
    high = payload[:, D].astype(jnp.float32)
    low = payload[:, D + 1].astype(jnp.float32)
    return high * 128.0 + low


def block_best(left_rows, left_labels, payload):
    scores = jnp.einsum("id,jd->ij", left_rows, payload[:, :D], preferred_element_type=jnp.float32)
    right_labels = tag_labels(payload)
    same_cluster = jnp.floor(left_labels[:, None] / ORDER_SPAN) == jnp.floor(right_labels[None, :] / ORDER_SPAN)
    earlier = same_cluster & (right_labels[None, :] < left_labels[:, None])
    return jnp.max(jnp.where(earlier, scores, jnp.float32(-1.0)), axis=1)


def partner_pairs(group_count, mask):
    return [(g, g ^ mask) for g in range(group_count)]


def per_device(embeddings, cluster_ids, row_index):
    group_count = lax.axis_size("grp")
    block_count = lax.axis_size("blk")
    rows_here = embeddings.shape[0]
    widened = embeddings.astype(jnp.float32)
    square_sum = jnp.sum(widened * widened, axis=1, keepdims=True)
    scale = lax.rsqrt(square_sum / D + 1e-06)
    high = (cluster_ids * 64 + row_index // 128).astype(jnp.float32)[:, None]
    low = (row_index % 128).astype(jnp.float32)[:, None]
    column = jnp.arange(D + TAG_WIDTH)[None, :]
    padded = jnp.pad(widened, ((0, 0), (0, TAG_WIDTH)))
    tags = jnp.where(column == D, high, jnp.where(column == D + 1, low, 0.0))
    payload = jnp.where(column < D, padded * scale / math.sqrt(D), tags).astype(jnp.bfloat16)

    order = ring_order(block_count)
    forward = [(order[i], order[(i + 1) % block_count]) for i in range(block_count)]
    backward = [(dst, src) for src, dst in forward]
    half = rows_here // 2
    steps = block_count // 2

    def send(which, visiting, step):
        if step == steps and block_count % 2 == 0:
            visiting = visiting[:half] if which == 0 else visiting[half:]
        return lax.ppermute(visiting, "blk", forward if which == 0 else backward)

    chains = [[payload, None, [payload]], [payload, None, []]]
    if steps >= 1:
        for which, chain in enumerate(chains):
            chain[0] = send(which, chain[0], 1)
            chain[2].append(chain[0])

    if group_count == 4:
        across = lax.ppermute(payload, "grp", partner_pairs(group_count, 2))
        beside = lax.ppermute(payload, "grp", partner_pairs(group_count, 1))
        diagonal = lax.ppermute(across, "grp", partner_pairs(group_count, 1))
        segment_pairs = [partner_pairs(group_count, k) for k in range(1, 4)]
        left_payload = jnp.concatenate([payload, beside, across, diagonal], axis=0)
    else:
        shifted = [lax.ppermute(payload, "grp", [(g, (g + k) % group_count) for g in range(group_count)])
                   for k in range(1, group_count)]
        segment_pairs = [[(g, (g - k) % group_count) for g in range(group_count)] for k in range(1, group_count)]
        left_payload = jnp.concatenate([payload] + shifted, axis=0)
    left_labels = tag_labels(left_payload)
    left_rows = left_payload[:, :D]

    def fold(best, blocks):
        for block in blocks:
            tile = block_best(left_rows, left_labels, block)
            best = tile if best is None else jnp.maximum(best, tile)
        return best

    for step in range(2, steps + 1):
        for which, chain in enumerate(chains):
            visiting, best, pending = chain
            visiting = send(which, visiting, step)
            best = fold(best, pending)
            chain[0], chain[1], chain[2] = visiting, best, [visiting]
    if steps >= 1 and block_count % 2 == 0:
        chains[0][2] = [jnp.concatenate([chains[0][2][-1], chains[1][2][-1]], axis=0)] + chains[0][2][:-1]
        chains[1][2] = chains[1][2][:-1]
    best = None
    for _, chain_best, pending in chains:
        chain_best = fold(chain_best, pending)
        if chain_best is not None:
            best = chain_best if best is None else jnp.maximum(best, chain_best)

    best = best.reshape(group_count, rows_here)
    if group_count == 4:
        swapped = lax.ppermute(jnp.stack([best[1], best[3]]), "grp", partner_pairs(group_count, 1))
        mine = jnp.maximum(best[0], swapped[0])
        across = jnp.maximum(best[2], swapped[1])
        return jnp.maximum(mine, lax.ppermute(across, "grp", partner_pairs(group_count, 2)))
    result = best[0]
    for k, pairs in enumerate(segment_pairs, start=1):
        result = jnp.maximum(result, lax.ppermute(best[k], "grp", pairs))
    return result


def solution(mesh):
    return jax.shard_map(
        per_device,
        mesh=mesh,
        in_specs=(P(("grp", "blk"), None), P(("grp", "blk")), P(("grp", "blk"))),
        out_specs=P(("grp", "blk")),
        check_vma=False,
    )
```

```python
import math

import jax
import jax.numpy as jnp
from jax import lax
from jax.sharding import PartitionSpec as P

D = 4096
TAG_WIDTH = 128
ORDER_SPAN = 8192.0


def ring_order(count):
    if count % 2:
        return list(range(count))
    return [2 * k for k in range(count // 2)] + [2 * k + 1 for k in reversed(range(count // 2))]


def tag_labels(payload):
    high = payload[:, D].astype(jnp.float32)
    low = payload[:, D + 1].astype(jnp.float32)
    return high * 128.0 + low


def block_best(left_rows, left_labels, payload):
    scores = jnp.einsum("id,jd->ij", left_rows, payload[:, :D], preferred_element_type=jnp.float32)
    right_labels = tag_labels(payload)
    same_cluster = jnp.floor(left_labels[:, None] / ORDER_SPAN) == jnp.floor(right_labels[None, :] / ORDER_SPAN)
    earlier = same_cluster & (right_labels[None, :] < left_labels[:, None])
    return jnp.max(jnp.where(earlier, scores, jnp.float32(-1.0)), axis=1)


def partner_pairs(group_count, mask):
    return [(g, g ^ mask) for g in range(group_count)]


def per_device(embeddings, cluster_ids, row_index):
    group_count = lax.axis_size("grp")
    block_count = lax.axis_size("blk")
    rows_here = embeddings.shape[0]
    widened = embeddings.astype(jnp.float32)
    gram = jnp.einsum("id,jd->ij", embeddings, embeddings, preferred_element_type=jnp.float32)
    diagonal = lax.broadcasted_iota(jnp.int32, gram.shape, 0) == lax.broadcasted_iota(jnp.int32, gram.shape, 1)
    square_sum = jnp.sum(jnp.where(diagonal, gram, 0.0), axis=1, keepdims=True)
    scale = lax.rsqrt(square_sum / D + 1e-06)
    high = (cluster_ids * 64 + row_index // 128).astype(jnp.float32)[:, None]
    low = (row_index % 128).astype(jnp.float32)[:, None]
    column = jnp.arange(D + TAG_WIDTH)[None, :]
    padded = jnp.pad(widened, ((0, 0), (0, TAG_WIDTH)))
    tags = jnp.where(column == D, high, jnp.where(column == D + 1, low, 0.0))
    payload = jnp.where(column < D, padded * scale / math.sqrt(D), tags).astype(jnp.bfloat16)

    order = ring_order(block_count)
    forward = [(order[i], order[(i + 1) % block_count]) for i in range(block_count)]
    backward = [(dst, src) for src, dst in forward]
    half = rows_here // 2
    steps = block_count // 2

    def send(which, visiting, step):
        if step == steps and block_count % 2 == 0:
            visiting = visiting[:half] if which == 0 else visiting[half:]
        return lax.ppermute(visiting, "blk", forward if which == 0 else backward)

    chains = [[payload, None, [payload]], [payload, None, []]]
    if steps >= 1:
        for which, chain in enumerate(chains):
            chain[0] = send(which, chain[0], 1)
            chain[2].append(chain[0])

    if group_count == 4:
        across = lax.ppermute(payload, "grp", partner_pairs(group_count, 2))
        beside = lax.ppermute(payload, "grp", partner_pairs(group_count, 1))
        diagonal = lax.ppermute(across, "grp", partner_pairs(group_count, 1))
        segment_pairs = [partner_pairs(group_count, k) for k in range(1, 4)]
        left_payload = jnp.concatenate([payload, beside, across, diagonal], axis=0)
    else:
        shifted = [lax.ppermute(payload, "grp", [(g, (g + k) % group_count) for g in range(group_count)])
                   for k in range(1, group_count)]
        segment_pairs = [[(g, (g - k) % group_count) for g in range(group_count)] for k in range(1, group_count)]
        left_payload = jnp.concatenate([payload] + shifted, axis=0)
    left_labels = tag_labels(left_payload)
    left_rows = left_payload[:, :D]

    def fold(best, blocks):
        for block in blocks:
            tile = block_best(left_rows, left_labels, block)
            best = tile if best is None else jnp.maximum(best, tile)
        return best

    for step in range(2, steps + 1):
        for which, chain in enumerate(chains):
            visiting, best, pending = chain
            visiting = send(which, visiting, step)
            best = fold(best, pending)
            chain[0], chain[1], chain[2] = visiting, best, [visiting]
    if steps >= 1 and block_count % 2 == 0:
        chains[0][2] = [jnp.concatenate([chains[0][2][-1], chains[1][2][-1]], axis=0)] + chains[0][2][:-1]
        chains[1][2] = chains[1][2][:-1]
    best = None
    for _, chain_best, pending in chains:
        chain_best = fold(chain_best, pending)
        if chain_best is not None:
            best = chain_best if best is None else jnp.maximum(best, chain_best)

    best = best.reshape(group_count, rows_here)
    if group_count == 4:
        swapped = lax.ppermute(jnp.stack([best[1], best[3]]), "grp", partner_pairs(group_count, 1))
        mine = jnp.maximum(best[0], swapped[0])
        across = jnp.maximum(best[2], swapped[1])
        return jnp.maximum(mine, lax.ppermute(across, "grp", partner_pairs(group_count, 2)))
    result = best[0]
    for k, pairs in enumerate(segment_pairs, start=1):
        result = jnp.maximum(result, lax.ppermute(best[k], "grp", pairs))
    return result


def solution(mesh):
    return jax.shard_map(
        per_device,
        mesh=mesh,
        in_specs=(P(("grp", "blk"), None), P(("grp", "blk")), P(("grp", "blk"))),
        out_specs=P(("grp", "blk")),
        check_vma=False,
    )
```

```python
import math

import jax
import jax.numpy as jnp
from jax import lax
from jax.sharding import PartitionSpec as P

D = 4096
TAG_WIDTH = 128
ORDER_SPAN = 8192.0


def ring_order(count):
    if count % 2:
        return list(range(count))
    return [2 * k for k in range(count // 2)] + [2 * k + 1 for k in reversed(range(count // 2))]


def tag_labels(payload):
    high = payload[:, D].astype(jnp.float32)
    low = payload[:, D + 1].astype(jnp.float32)
    return high * 128.0 + low


def block_best(left_rows, left_labels, payload):
    scores = jnp.einsum("id,jd->ij", left_rows, payload[:, :D], preferred_element_type=jnp.float32)
    right_labels = tag_labels(payload)
    same_cluster = jnp.floor(left_labels[:, None] / ORDER_SPAN) == jnp.floor(right_labels[None, :] / ORDER_SPAN)
    earlier = same_cluster & (right_labels[None, :] < left_labels[:, None])
    return jnp.max(jnp.where(earlier, scores, jnp.float32(-1.0)), axis=1)


def partner_pairs(group_count, mask):
    return [(g, g ^ mask) for g in range(group_count)]


def per_device(embeddings, cluster_ids, row_index):
    group_count = lax.axis_size("grp")
    block_count = lax.axis_size("blk")
    rows_here = embeddings.shape[0]
    widened = embeddings.astype(jnp.float32)
    square_sum = jnp.sum(widened * widened, axis=1, keepdims=True)
    scale = lax.rsqrt(square_sum / D + 1e-06)
    high = (cluster_ids * 64 + row_index // 128).astype(jnp.float32)[:, None]
    low = (row_index % 128).astype(jnp.float32)[:, None]
    column = jnp.arange(D + TAG_WIDTH)[None, :]
    padded = jnp.pad(widened, ((0, 0), (0, TAG_WIDTH)))
    tags = jnp.where(column == D, high, jnp.where(column == D + 1, low, 0.0))
    payload = jnp.where(column < D, padded * scale / math.sqrt(D), tags).astype(jnp.bfloat16)

    order = ring_order(block_count)
    forward = [(order[i], order[(i + 1) % block_count]) for i in range(block_count)]
    backward = [(dst, src) for src, dst in forward]
    half = rows_here // 2
    steps = block_count // 2

    def send(which, visiting, step):
        if step == steps and block_count % 2 == 0:
            visiting = visiting[:half] if which == 0 else visiting[half:]
        return lax.ppermute(visiting, "blk", forward if which == 0 else backward)

    chains = [[payload, None, [payload]], [payload, None, []]]
    if steps >= 1:
        for which, chain in enumerate(chains):
            chain[0] = send(which, chain[0], 1)
            chain[2].append(chain[0])

    if group_count == 4:
        across = lax.ppermute(payload, "grp", partner_pairs(group_count, 2))
        beside = lax.ppermute(payload, "grp", partner_pairs(group_count, 1))
        diagonal = lax.ppermute(across, "grp", partner_pairs(group_count, 1))
        segment_pairs = [partner_pairs(group_count, k) for k in range(1, 4)]
        left_payload = jnp.concatenate([payload, beside, across, diagonal], axis=0)
    else:
        shifted = [lax.ppermute(payload, "grp", [(g, (g + k) % group_count) for g in range(group_count)])
                   for k in range(1, group_count)]
        segment_pairs = [[(g, (g - k) % group_count) for g in range(group_count)] for k in range(1, group_count)]
        left_payload = jnp.concatenate([payload] + shifted, axis=0)
    left_labels = tag_labels(left_payload)
    left_rows = left_payload[:, :D]

    def fold(best, blocks):
        for block in blocks:
            tile = block_best(left_rows, left_labels, block)
            best = tile if best is None else jnp.maximum(best, tile)
        return best

    def fold_joined(best, blocks):
        if not blocks:
            return best
        joined = blocks[0] if len(blocks) == 1 else jnp.concatenate(blocks, axis=0)
        tile = block_best(left_rows, left_labels, joined)
        return tile if best is None else jnp.maximum(best, tile)

    best = None
    for step in range(2, steps + 1):
        pending = chains[0][2] + chains[1][2]
        for which, chain in enumerate(chains):
            chain[0] = send(which, chain[0], step)
            chain[2] = [chain[0]]
        best = fold_joined(best, pending)
    if steps >= 1 and block_count % 2 == 0:
        last = [chains[0][2][-1], chains[1][2][-1]]
        rest = chains[0][2][:-1] + chains[1][2][:-1]
    else:
        last, rest = chains[0][2] + chains[1][2], []
    best = fold_joined(best, rest)
    best = fold_joined(best, last)

    best = best.reshape(group_count, rows_here)
    if group_count == 4:
        swapped = lax.ppermute(jnp.stack([best[1], best[3]]), "grp", partner_pairs(group_count, 1))
        mine = jnp.maximum(best[0], swapped[0])
        across = jnp.maximum(best[2], swapped[1])
        return jnp.maximum(mine, lax.ppermute(across, "grp", partner_pairs(group_count, 2)))
    result = best[0]
    for k, pairs in enumerate(segment_pairs, start=1):
        result = jnp.maximum(result, lax.ppermute(best[k], "grp", pairs))
    return result


def solution(mesh):
    return jax.shard_map(
        per_device,
        mesh=mesh,
        in_specs=(P(("grp", "blk"), None), P(("grp", "blk")), P(("grp", "blk"))),
        out_specs=P(("grp", "blk")),
        check_vma=False,
    )
```

```python
import math

import jax
import jax.numpy as jnp
from jax import lax
from jax.sharding import PartitionSpec as P

D = 4096
TAG_WIDTH = 128
ORDER_SPAN = 8192.0


def ring_order(count):
    if count % 2:
        return list(range(count))
    return [2 * k for k in range(count // 2)] + [2 * k + 1 for k in reversed(range(count // 2))]


def tag_labels(payload):
    high = payload[:, D].astype(jnp.float32)
    low = payload[:, D + 1].astype(jnp.float32)
    return high * 128.0 + low


def block_best(left_rows, left_labels, payload):
    scores = jnp.einsum("id,jd->ij", left_rows, payload[:, :D], preferred_element_type=jnp.float32)
    right_labels = tag_labels(payload)
    same_cluster = jnp.floor(left_labels[:, None] / ORDER_SPAN) == jnp.floor(right_labels[None, :] / ORDER_SPAN)
    earlier = same_cluster & (right_labels[None, :] < left_labels[:, None])
    return jnp.max(jnp.where(earlier, scores, jnp.float32(-1.0)), axis=1)


def partner_pairs(group_count, mask):
    return [(g, g ^ mask) for g in range(group_count)]


def per_device(embeddings, cluster_ids, row_index):
    group_count = lax.axis_size("grp")
    block_count = lax.axis_size("blk")
    rows_here = embeddings.shape[0]
    widened = embeddings.astype(jnp.float32)
    square_sum = jnp.sum(widened * widened, axis=1, keepdims=True)
    scale = lax.rsqrt(square_sum / D + 1e-06)
    high = (cluster_ids * 64 + row_index // 128).astype(jnp.float32)[:, None]
    low = (row_index % 128).astype(jnp.float32)[:, None]
    column = jnp.arange(D + TAG_WIDTH)[None, :]
    padded = jnp.pad(widened, ((0, 0), (0, TAG_WIDTH)))
    tags = jnp.where(column == D, high, jnp.where(column == D + 1, low, 0.0))
    payload = jnp.where(column < D, padded * scale / math.sqrt(D), tags).astype(jnp.bfloat16)

    order = ring_order(block_count)
    forward = [(order[i], order[(i + 1) % block_count]) for i in range(block_count)]
    backward = [(dst, src) for src, dst in forward]
    half = min(rows_here, (rows_here * 5 // 8) // 8 * 8)
    steps = block_count // 2

    def send(which, visiting, step):
        if step == steps and block_count % 2 == 0:
            visiting = visiting[:half] if which == 0 else visiting[half:]
        return lax.ppermute(visiting, "blk", forward if which == 0 else backward)

    chains = [[payload, None, [payload]], [payload, None, []]]
    if steps >= 1:
        for which, chain in enumerate(chains):
            chain[0] = send(which, chain[0], 1)
            chain[2].append(chain[0])

    if group_count == 4:
        across = lax.ppermute(payload, "grp", partner_pairs(group_count, 2))
        beside = lax.ppermute(payload, "grp", partner_pairs(group_count, 1))
        diagonal = lax.ppermute(across, "grp", partner_pairs(group_count, 1))
        segment_pairs = [partner_pairs(group_count, k) for k in range(1, 4)]
        left_payload = jnp.concatenate([payload, beside, across, diagonal], axis=0)
    else:
        shifted = [lax.ppermute(payload, "grp", [(g, (g + k) % group_count) for g in range(group_count)])
                   for k in range(1, group_count)]
        segment_pairs = [[(g, (g - k) % group_count) for g in range(group_count)] for k in range(1, group_count)]
        left_payload = jnp.concatenate([payload] + shifted, axis=0)
    left_labels = tag_labels(left_payload)
    left_rows = left_payload[:, :D]

    def fold(best, blocks):
        for block in blocks:
            tile = block_best(left_rows, left_labels, block)
            best = tile if best is None else jnp.maximum(best, tile)
        return best

    for step in range(2, steps + 1):
        for which, chain in enumerate(chains):
            visiting, best, pending = chain
            visiting = send(which, visiting, step)
            best = fold(best, pending)
            chain[0], chain[1], chain[2] = visiting, best, [visiting]
    if steps >= 1 and block_count % 2 == 0:
        chains[0][2] = [jnp.concatenate([chains[0][2][-1], chains[1][2][-1]], axis=0)] + chains[0][2][:-1]
        chains[1][2] = chains[1][2][:-1]
    best = None
    for _, chain_best, pending in chains:
        chain_best = fold(chain_best, pending)
        if chain_best is not None:
            best = chain_best if best is None else jnp.maximum(best, chain_best)

    best = best.reshape(group_count, rows_here)
    if group_count == 4:
        swapped = lax.ppermute(jnp.stack([best[1], best[3]]), "grp", partner_pairs(group_count, 1))
        mine = jnp.maximum(best[0], swapped[0])
        across = jnp.maximum(best[2], swapped[1])
        return jnp.maximum(mine, lax.ppermute(across, "grp", partner_pairs(group_count, 2)))
    result = best[0]
    for k, pairs in enumerate(segment_pairs, start=1):
        result = jnp.maximum(result, lax.ppermute(best[k], "grp", pairs))
    return result


def solution(mesh):
    return jax.shard_map(
        per_device,
        mesh=mesh,
        in_specs=(P(("grp", "blk"), None), P(("grp", "blk")), P(("grp", "blk"))),
        out_specs=P(("grp", "blk")),
        check_vma=False,
    )
```

```python
import math

import jax
import jax.numpy as jnp
from jax import lax
from jax.sharding import PartitionSpec as P

D = 4096
TAG_WIDTH = 128
ORDER_SPAN = 8192.0


def ring_order(count):
    if count % 2:
        return list(range(count))
    return [2 * k for k in range(count // 2)] + [2 * k + 1 for k in reversed(range(count // 2))]


def tag_labels(payload):
    high = payload[:, D].astype(jnp.float32)
    low = payload[:, D + 1].astype(jnp.float32)
    return high * 128.0 + low


def block_best(left_rows, left_labels, payload):
    scores = jnp.einsum("id,jd->ij", left_rows, payload[:, :D], preferred_element_type=jnp.float32)
    right_labels = tag_labels(payload)
    same_cluster = jnp.floor(left_labels[:, None] / ORDER_SPAN) == jnp.floor(right_labels[None, :] / ORDER_SPAN)
    earlier = same_cluster & (right_labels[None, :] < left_labels[:, None])
    return jnp.max(jnp.where(earlier, scores, jnp.float32(-1.0)), axis=1)


def partner_pairs(group_count, mask):
    return [(g, g ^ mask) for g in range(group_count)]


def per_device(embeddings, cluster_ids, row_index):
    group_count = lax.axis_size("grp")
    block_count = lax.axis_size("blk")
    rows_here = embeddings.shape[0]
    padded = jnp.pad(embeddings, ((0, 0), (0, TAG_WIDTH))).astype(jnp.float32)
    square_sum = jnp.sum(padded * padded, axis=1, keepdims=True)
    scale = lax.rsqrt(square_sum / D + 1e-06)
    high = (cluster_ids * 64 + row_index // 128).astype(jnp.float32)[:, None]
    low = (row_index % 128).astype(jnp.float32)[:, None]
    column = jnp.arange(D + TAG_WIDTH)[None, :]
    tags = jnp.where(column == D, high, jnp.where(column == D + 1, low, 0.0))
    payload = jnp.where(column < D, padded * scale / math.sqrt(D), tags).astype(jnp.bfloat16)

    order = ring_order(block_count)
    forward = [(order[i], order[(i + 1) % block_count]) for i in range(block_count)]
    backward = [(dst, src) for src, dst in forward]
    half = min(rows_here, (rows_here * 5 // 8) // 8 * 8)
    steps = block_count // 2

    def send(which, visiting, step):
        if step == steps and block_count % 2 == 0:
            visiting = visiting[:half] if which == 0 else visiting[half:]
        return lax.ppermute(visiting, "blk", forward if which == 0 else backward)

    chains = [[payload, None, [payload]], [payload, None, []]]
    if steps >= 1:
        for which, chain in enumerate(chains):
            chain[0] = send(which, chain[0], 1)
            chain[2].append(chain[0])

    if group_count == 4:
        across = lax.ppermute(payload, "grp", partner_pairs(group_count, 2))
        beside = lax.ppermute(payload, "grp", partner_pairs(group_count, 1))
        diagonal = lax.ppermute(across, "grp", partner_pairs(group_count, 1))
        segment_pairs = [partner_pairs(group_count, k) for k in range(1, 4)]
        left_payload = jnp.concatenate([payload, beside, across, diagonal], axis=0)
    else:
        shifted = [lax.ppermute(payload, "grp", [(g, (g + k) % group_count) for g in range(group_count)])
                   for k in range(1, group_count)]
        segment_pairs = [[(g, (g - k) % group_count) for g in range(group_count)] for k in range(1, group_count)]
        left_payload = jnp.concatenate([payload] + shifted, axis=0)
    left_labels = tag_labels(left_payload)
    left_rows = left_payload[:, :D]

    def fold(best, blocks):
        for block in blocks:
            tile = block_best(left_rows, left_labels, block)
            best = tile if best is None else jnp.maximum(best, tile)
        return best

    for step in range(2, steps + 1):
        for which, chain in enumerate(chains):
            visiting, best, pending = chain
            visiting = send(which, visiting, step)
            best = fold(best, pending)
            chain[0], chain[1], chain[2] = visiting, best, [visiting]
    if steps >= 1 and block_count % 2 == 0:
        chains[0][2] = [jnp.concatenate([chains[0][2][-1], chains[1][2][-1]], axis=0)] + chains[0][2][:-1]
        chains[1][2] = chains[1][2][:-1]
    best = None
    for _, chain_best, pending in chains:
        chain_best = fold(chain_best, pending)
        if chain_best is not None:
            best = chain_best if best is None else jnp.maximum(best, chain_best)

    best = best.reshape(group_count, rows_here)
    if group_count == 4:
        swapped = lax.ppermute(jnp.stack([best[1], best[3]]), "grp", partner_pairs(group_count, 1))
        mine = jnp.maximum(best[0], swapped[0])
        across = jnp.maximum(best[2], swapped[1])
        return jnp.maximum(mine, lax.ppermute(across, "grp", partner_pairs(group_count, 2)))
    result = best[0]
    for k, pairs in enumerate(segment_pairs, start=1):
        result = jnp.maximum(result, lax.ppermute(best[k], "grp", pairs))
    return result


def solution(mesh):
    return jax.shard_map(
        per_device,
        mesh=mesh,
        in_specs=(P(("grp", "blk"), None), P(("grp", "blk")), P(("grp", "blk"))),
        out_specs=P(("grp", "blk")),
        check_vma=False,
    )
```
